128 devices in a mesh: line: 64 (over z, y, x), tile: 2 (over core).
Axes of the slice: x: 4, y: 4, z: 4, core: 2. Of those that a mesh axis runs over, the one named last changes fastest.
Arguments:
- traces: bfloat16 [32768, 2048], P(('line', 'tile')), may hold values from -6 to 6
- trace_line: int32 [32768], P(('line', 'tile')), may hold values from 0 to 63, as said below
- trace_bin: int32 [32768], P(('line', 'tile')), may hold values from 0 to 127, as said below
- block_offset: int32 [256], P(('line', 'tile')), may hold values from 0 to 3
- nmo_coef: bfloat16 [64, 4, 8, 2048], P('line'), may hold values from -4 to 4
- band_shift: int32 [64, 4, 2048], P('line'), may hold values from 0 to 120
- bandpass: float32 [31, 2048], replicated, may hold values from -1 to 1
- fold: int32 [64, 128], P('line', 'tile'), may hold values from 4 to 20
Outputs:
- stack: float32 [64, 128, 2048], P('line', 'tile')
The draws below stay inside these ranges and needn't reach their ends.
Inputs may be any that keep to these rules, and one draw needn't show every extreme that they name: `trace_line`: of one reader device's 256 traces at most 8 go to one line, and in every draw each device sends exactly 8 to some line. `trace_bin`: the bins of a line form 2 tiles of 64 consecutive bins; of one reader device's traces at most 4 go to one tile of one line, and in every draw each device sends exactly 4 to some tile of some line.
All inputs are finite; a program needn't handle non-finite values.
Results may differ from the reference program's by a relative error of at most 0.0003.
Values may be sent and summed in bfloat16 or wider, within the bound.
No kernel may reach another device: no remote copies, remote signals or barrier semaphores. Data moves between devices by JAX's collectives and lax.ppermute only.
A program may use at most 64 MiB of HBM per device.

```python
import jax
import jax.numpy as jnp
from jax import lax

NT = 2048
BLK = 128
NOFF = 4
BW = 8
SHIFT = 120
FL = 31
BINS = 128
TR_DEV = 256
TRACES = 32768
CAP = 8
CAPT = 4
BIN_TILE = 64
LINES = 64
N_LINE = 64
N_TILE = 2


def geometry(key):
    readers = N_LINE * N_TILE
    cells = N_LINE * CAP
    heavy = jax.random.randint(jax.random.fold_in(key, 11), (N_LINE,), 0, 4)

    def one_reader(reader_key):
        key_a, key_b, key_c, key_d, key_e = jax.random.split(reader_key, 5)
        forced = jax.random.randint(key_a, (), 0, N_LINE)
        noise = jax.random.randint(key_b, (N_LINE, CAP), 0, 4096)
        line_grid = jnp.broadcast_to(jnp.arange(N_LINE, dtype=jnp.int32)[:, None], (N_LINE, CAP))
        score = noise * (1 + heavy[:, None]) + jnp.where(line_grid == forced, 16384, 0)
        score = score.reshape(-1) * cells + jnp.arange(cells, dtype=jnp.int32)
        chosen = lax.top_k(score, TR_DEV)[1]
        chosen = chosen[jax.random.permutation(key_c, TR_DEV)]
        line_index = chosen // CAP
        slot_index = chosen % CAP
        tile_orders = jax.vmap(lambda line_key: jax.random.permutation(line_key, N_TILE))(jax.random.split(key_d, N_LINE))
        tile_index = tile_orders[line_index, slot_index // CAPT]
        within = jax.random.randint(key_e, (TR_DEV,), 0, BIN_TILE)
        return (line_index, tile_index * BIN_TILE + within)
    keys = jax.random.split(jax.random.fold_in(key, 5), readers)
    lines, bins_drawn = jax.vmap(one_reader)(keys)
    return (lines.reshape(-1).astype(jnp.int32), bins_drawn.reshape(-1).astype(jnp.int32))


def draw_trace_line(key, part):
    return geometry(key)[0]


def draw_trace_bin(key, part):
    return geometry(key)[1]


def with_ends(entries, key, low, largest):
    longest = entries.shape.index(max(entries.shape))
    spots = []
    for shift in (0, 1):
        where = [jax.random.randint(jax.random.fold_in(key, axis), (), 0, length) for axis, length in enumerate(entries.shape)]
        where[longest] = (where[longest] + shift) % entries.shape[longest]
        spots.append(tuple(where))
    return entries.at[spots[0]].set(low).at[spots[1]].set(largest)


def block_levels(own_key, shape, pieces, low, high):
    loudness, own = 1.0, jax.random.fold_in(own_key, 6)
    for dim, blocks in pieces:
        draws = jnp.exp(jax.random.uniform(jax.random.fold_in(own, dim), (blocks,), jnp.float32, low / len(pieces), high / len(pieces)))
        loudness = loudness * jnp.repeat(draws, shape[dim] // blocks).reshape([-1 if axis == dim else 1 for axis in range(len(shape))])
    return loudness


def gaussian(own_key, extent, width, reach, cuts=(), kind=jnp.bfloat16):
    entries = width * jax.random.normal(own_key, extent, jnp.float32)
    if cuts:
        entries = entries * block_levels(own_key, extent, cuts, -0.22, 0.18)
    return jnp.clip(entries, -reach, reach).astype(kind)


def setup_inputs(seed: int = 0) -> dict:
    seeds = jax.random.split(jax.random.key(seed), 9)
    traces = gaussian(seeds[0], (TRACES, NT), 1.0, 6.0, ((0, 128),))
    trace_line = draw_trace_line(jax.random.fold_in(seeds[8], 71), 0)
    trace_bin = draw_trace_bin(jax.random.fold_in(seeds[8], 71), 0)
    block_offset = with_ends(jax.random.randint(seeds[3], (TRACES // BLK,), 0, NOFF), jax.random.fold_in(seeds[3], 1), 0, NOFF - 1).astype(jnp.int32)
    nmo_coef = gaussian(seeds[4], (LINES, NOFF, BW, NT), 0.6, 4.0, ((0, 64),))
    band_shift = with_ends(jax.random.randint(seeds[5], (LINES, NOFF, NT), 0, SHIFT + 1), jax.random.fold_in(seeds[5], 1), 0, SHIFT).astype(jnp.int32)
    bandpass = gaussian(seeds[6], (FL, NT), FL ** -0.5, 1.0, (), jnp.float32)
    fold = with_ends(jax.random.randint(seeds[7], (LINES, BINS), 4, 21), jax.random.fold_in(seeds[7], 1), 4, 20).astype(jnp.int32)
    return {"traces": traces, "trace_line": trace_line, "trace_bin": trace_bin, "block_offset": block_offset, "nmo_coef": nmo_coef, "band_shift": band_shift, "bandpass": bandpass, "fold": fold}


def reference(traces, trace_line, trace_bin, block_offset, nmo_coef, band_shift, bandpass, fold):
    block_total = block_offset.shape[0]
    blocks = traces.reshape(block_total, BLK, NT)
    line_blocks = trace_line.reshape(block_total, BLK)
    bin_blocks = trace_bin.reshape(block_total, BLK)
    tap_iota = jnp.arange(BW, dtype=jnp.int32)
    sample_iota = jnp.arange(NT, dtype=jnp.int32)

    def step(total, items):
        block, line_ids, bin_ids, offset_class = items
        weights = nmo_coef[line_ids, offset_class].astype(jnp.float32)
        shifts = band_shift[line_ids, offset_class].astype(jnp.int32)
        index = sample_iota[None, None, :] + shifts[:, None, :] + tap_iota[None, :, None]
        padded = jnp.concatenate([block.astype(jnp.float32), jnp.zeros((BLK, 128), jnp.float32)], 1)
        spread = jnp.broadcast_to(padded[:, None, :], (BLK, BW, NT + 128))
        values = jnp.take_along_axis(spread, index.astype(jnp.int32), axis=2)
        corrected = jnp.sum(weights * values, axis=1)
        total = total.at[(line_ids * BINS + bin_ids).astype(jnp.int32)].add(corrected)
        return total, None

    start = jnp.zeros((N_LINE * BINS, NT), jnp.float32)
    gathered, _ = lax.scan(step, start, (blocks, line_blocks, bin_blocks, block_offset))
    half = (FL - 1) // 2
    padded_stack = jnp.concatenate([jnp.zeros((N_LINE * BINS, half), jnp.float32), gathered, jnp.zeros((N_LINE * BINS, FL - 1 - half), jnp.float32)], 1)
    filtered = jnp.zeros((N_LINE * BINS, NT), jnp.float32)
    for tap_index in range(FL):
        filtered = filtered + bandpass[tap_index][None, :] * padded_stack[:, tap_index:tap_index + NT]
    result = filtered / fold.reshape(-1).astype(jnp.float32)[:, None]
    return result.reshape(N_LINE, BINS, NT)
```

```python
import jax
import jax.numpy as jnp
from jax import lax
from jax.sharding import PartitionSpec as P

META = 128


def windows(data, left):
    rows_count = data.shape[0]
    length = data.shape[1]
    groups = length // 128
    padded = jnp.concatenate(
        [
            jnp.zeros((rows_count, left), data.dtype),
            data,
            jnp.zeros((rows_count, 256 - left), data.dtype),
        ],
        1,
    )
    first = padded[:, :length].reshape(rows_count, groups, 128)
    second = padded[:, 128 : length + 128].reshape(rows_count, groups, 128)
    return jnp.concatenate([first, second], 2)


def moveout_matrix(coef_rows, shift_rows):
    taps_count = coef_rows.shape[0]
    groups = coef_rows.shape[1] // 128
    column = jnp.arange(128, dtype=jnp.int32).reshape(1, 1, 128)
    position = jnp.arange(256, dtype=jnp.int32).reshape(1, 256, 1)
    shifts = shift_rows.reshape(groups, 1, 128)
    weights = coef_rows.astype(jnp.float32).reshape(taps_count, groups, 1, 128)
    matrix = jnp.zeros((groups, 256, 128), jnp.float32)
    for tap_index in range(taps_count):
        matrix = matrix + jnp.where(
            position == column + shifts + tap_index, weights[tap_index], 0.0
        )
    return matrix.astype(jnp.bfloat16)


def bandpass_matrix(taps):
    taps_count = taps.shape[0]
    groups = taps.shape[1] // 128
    half = (taps_count - 1) // 2
    column = jnp.arange(128, dtype=jnp.int32).reshape(1, 1, 128)
    position = jnp.arange(256, dtype=jnp.int32).reshape(1, 256, 1)
    weights = taps.reshape(taps_count, groups, 1, 128)
    matrix = jnp.zeros((groups, 256, 128), jnp.float32)
    for tap_index in range(taps_count):
        matrix = matrix + jnp.where(
            position == column + 64 + tap_index - half, weights[tap_index], 0.0
        )
    return matrix


def apply_filter(stacked, matrix):
    rows_count = stacked.shape[0]
    result = jnp.einsum(
        "rgw,gwc->rgc",
        windows(stacked, 64),
        matrix,
        precision=lax.Precision.HIGHEST,
        preferred_element_type=jnp.float32,
    )
    return result.reshape(rows_count, -1)


def moveout(rows, slot_class, nmo_coef, band_shift):
    slot_count, length = rows.shape
    window_rows = windows(rows, 0)
    corrected = jnp.zeros((slot_count, length // 128, 128), jnp.float32)
    for offset_index in range(nmo_coef.shape[1]):
        matrix = moveout_matrix(nmo_coef[0, offset_index], band_shift[0, offset_index])
        product = jnp.einsum(
            "sgw,gwc->sgc", window_rows, matrix, preferred_element_type=jnp.float32
        )
        corrected = corrected + jnp.where((slot_class == offset_index)[:, None, None], product, 0.0)
    return corrected.reshape(slot_count, length)


def ranks(keys, key_count):
    onehot = (keys[:, None] == jnp.arange(key_count, dtype=jnp.int32)[None, :]).astype(jnp.int32)
    running = jnp.cumsum(onehot, 0)
    return jnp.sum(onehot * running, 1) - 1


def body(traces, trace_line, trace_bin, block_offset, nmo_coef, band_shift, bandpass, fold):
    line_count = lax.axis_size("line")
    tile_count = lax.axis_size("tile")
    trace_count, length = traces.shape
    block_rows = trace_count // block_offset.shape[0]
    bin_share = fold.shape[1]
    dest_count = line_count * tile_count
    capacity = 4
    slots = dest_count * capacity
    trace_class = jnp.repeat(block_offset, block_rows)
    trace_tile = trace_bin // bin_share
    dest = trace_line * tile_count + trace_tile
    slot_of_trace = dest * capacity + ranks(dest, dest_count)
    lane = jnp.arange(META, dtype=jnp.int32)[None, :]
    meta_block = jnp.where(
        lane == 0,
        (trace_bin % bin_share)[:, None],
        jnp.where(lane == 1, trace_class[:, None], jnp.where(lane == 2, 1, 0)),
    ).astype(jnp.bfloat16)
    extended = jnp.concatenate([traces, meta_block], 1)
    select = (
        jnp.arange(slots, dtype=jnp.int32)[:, None] == slot_of_trace[None, :]
    ).astype(jnp.bfloat16)
    send = jnp.dot(select, extended, preferred_element_type=jnp.float32).astype(jnp.bfloat16)
    received = lax.all_to_all(
        send.reshape(dest_count, capacity, length + META),
        ("line", "tile"),
        split_axis=0,
        concat_axis=0,
        tiled=True,
    ).reshape(slots, length + META)
    rows = received[:, :length]
    meta = received[:, length:length + 3].astype(jnp.int32)
    valid = meta[:, 2] == 1
    slot_bin = jnp.where(valid, meta[:, 0], -1)
    slot_class = jnp.where(valid, meta[:, 1], -1)
    corrected = moveout(rows, slot_class, nmo_coef, band_shift)
    selector = (jnp.arange(bin_share, dtype=jnp.int32)[:, None] == slot_bin[None, :]).astype(
        jnp.float32
    )
    stacked = jnp.dot(
        selector, corrected, precision=lax.Precision.HIGHEST, preferred_element_type=jnp.float32
    )
    filtered = apply_filter(stacked, bandpass_matrix(bandpass))
    fold_share = fold[0].astype(jnp.float32)[:, None]
    return (filtered / fold_share)[None]


def solution(mesh):
    placed = (
        P(("line", "tile"), None),
        P(("line", "tile")),
        P(("line", "tile")),
        P(("line", "tile")),
        P("line", None, None, None),
        P("line", None, None),
        P(),
        P("line", "tile"),
    )
    return jax.shard_map(
        body, mesh=mesh, in_specs=placed, out_specs=P("line", "tile", None), check_vma=False
    )
```

```python
import jax
import jax.numpy as jnp
from jax import lax
from jax.sharding import PartitionSpec as P
from jax.experimental import pallas as pl

META = 128


def moveout_matrix(coef_rows, shift_rows):
    taps_count = coef_rows.shape[0]
    groups = coef_rows.shape[1] // 128
    column = jnp.arange(128, dtype=jnp.int32).reshape(1, 1, 128)
    position = jnp.arange(256, dtype=jnp.int32).reshape(1, 256, 1)
    shifts = shift_rows.reshape(groups, 1, 128)
    weights = coef_rows.astype(jnp.float32).reshape(taps_count, groups, 1, 128)
    matrix = jnp.zeros((groups, 256, 128), jnp.float32)
    for tap_index in range(taps_count):
        matrix = matrix + jnp.where(
            position == column + shifts + tap_index, weights[tap_index], 0.0
        )
    return matrix.astype(jnp.bfloat16)


def bandpass_matrix(taps):
    taps_count = taps.shape[0]
    groups = taps.shape[1] // 128
    half = (taps_count - 1) // 2
    column = jnp.arange(128, dtype=jnp.int32).reshape(1, 1, 128)
    position = jnp.arange(384, dtype=jnp.int32).reshape(1, 384, 1)
    weights = taps.reshape(taps_count, groups, 1, 128)
    matrix = jnp.zeros((groups, 384, 128), jnp.float32)
    for tap_index in range(taps_count):
        matrix = matrix + jnp.where(
            position == column + 128 + tap_index - half, weights[tap_index], 0.0
        )
    return matrix


def split3(value):
    high = value.astype(jnp.bfloat16)
    rest = value - high.astype(jnp.float32)
    middle = rest.astype(jnp.bfloat16)
    low = (rest - middle.astype(jnp.float32)).astype(jnp.bfloat16)
    return high, middle, low


def dot32(left, right):
    a = split3(left)
    b = split3(right)
    pairs = ((0, 0), (0, 1), (1, 0), (0, 2), (2, 0), (1, 1))
    total = None
    for i, j in pairs:
        part = jnp.dot(a[i], b[j], preferred_element_type=jnp.float32)
        total = part if total is None else total + part
    return total


def moveout_kernel(rows_ref, class_ref, select_ref, matrix_ref, out_ref):
    group = pl.program_id(0)
    length = out_ref.shape[1] * pl.num_programs(0)
    start = pl.multiple_of(group * 128, 128)
    window = rows_ref[:, pl.ds(start, 256)]
    lanes = start + lax.broadcasted_iota(jnp.int32, (1, 256), 1)
    window = jnp.where(lanes < length, window, jnp.zeros((), window.dtype))
    slot_class = class_ref[...]
    corrected = jnp.zeros((window.shape[0], 128), jnp.float32)
    for offset_index in range(matrix_ref.shape[0]):
        product = jnp.dot(window, matrix_ref[offset_index, 0], preferred_element_type=jnp.float32)
        corrected = corrected + jnp.where(slot_class == offset_index, product, 0.0)
    select = select_ref[...]
    total = None
    for part in split3(corrected):
        piece = jnp.dot(select, part, preferred_element_type=jnp.float32)
        total = piece if total is None else total + piece
    out_ref[...] = total


def filter_kernel(stack_ref, matrix_ref, fold_ref, out_ref):
    group = pl.program_id(0)
    groups = pl.num_programs(0)
    total = None
    for step in range(3):
        index = group + step - 1
        clipped = jnp.clip(index, 0, groups - 1)
        block = stack_ref[:, pl.ds(pl.multiple_of(clipped * 128, 128), 128)]
        keep = jnp.logical_and(index >= 0, index < groups)
        block = jnp.where(keep, block, 0.0)
        piece = dot32(block, matrix_ref[0, step * 128:(step + 1) * 128, :])
        total = piece if total is None else total + piece
    out_ref[...] = total / fold_ref[...]


def moveout_stack(rows, slot_class, select, matrices, length):
    slot_count, width = rows.shape
    bins = select.shape[0]
    classes, groups = matrices.shape[0], matrices.shape[1]
    return pl.pallas_call(
        moveout_kernel,
        grid=(groups,),
        in_specs=[
            pl.BlockSpec((slot_count, width), lambda g: (0, 0)),
            pl.BlockSpec((slot_count, 1), lambda g: (0, 0)),
            pl.BlockSpec((bins, slot_count), lambda g: (0, 0)),
            pl.BlockSpec((classes, 1, 256, 128), lambda g: (0, g, 0, 0)),
        ],
        out_specs=pl.BlockSpec((bins, 128), lambda g: (0, g)),
        out_shape=jax.ShapeDtypeStruct((bins, length), jnp.float32),
    )(rows, slot_class, select, matrices)


def filter_stack(stacked, matrix, fold_share):
    bins, length = stacked.shape
    groups = matrix.shape[0]
    return pl.pallas_call(
        filter_kernel,
        grid=(groups,),
        in_specs=[
            pl.BlockSpec((bins, length), lambda g: (0, 0)),
            pl.BlockSpec((1, 384, 128), lambda g: (g, 0, 0)),
            pl.BlockSpec((bins, 1), lambda g: (0, 0)),
        ],
        out_specs=pl.BlockSpec((bins, 128), lambda g: (0, g)),
        out_shape=jax.ShapeDtypeStruct((bins, length), jnp.float32),
    )(stacked, matrix, fold_share)


def ranks(keys, key_count):
    onehot = (keys[:, None] == jnp.arange(key_count, dtype=jnp.int32)[None, :]).astype(jnp.int32)
    running = jnp.cumsum(onehot, 0)
    return jnp.sum(onehot * running, 1) - 1


def body(traces, trace_line, trace_bin, block_offset, nmo_coef, band_shift, bandpass, fold):
    line_count = lax.axis_size("line")
    tile_count = lax.axis_size("tile")
    trace_count, length = traces.shape
    block_rows = trace_count // block_offset.shape[0]
    bin_share = fold.shape[1]
    dest_count = line_count * tile_count
    capacity = 4
    slots = dest_count * capacity
    trace_class = jnp.repeat(block_offset, block_rows)
    trace_tile = trace_bin // bin_share
    dest = trace_line * tile_count + trace_tile
    slot_of_trace = dest * capacity + ranks(dest, dest_count)
    lane = jnp.arange(META, dtype=jnp.int32)[None, :]
    meta_block = jnp.where(
        lane == 0,
        (trace_bin % bin_share)[:, None],
        jnp.where(lane == 1, trace_class[:, None], jnp.where(lane == 2, 1, 0)),
    ).astype(jnp.bfloat16)
    extended = jnp.concatenate([traces, meta_block], 1)
    select = (
        jnp.arange(slots, dtype=jnp.int32)[:, None] == slot_of_trace[None, :]
    ).astype(jnp.bfloat16)
    send = jnp.dot(select, extended, preferred_element_type=jnp.float32).astype(jnp.bfloat16)
    received = lax.all_to_all(
        send.reshape(dest_count, capacity, length + META),
        ("line", "tile"),
        split_axis=0,
        concat_axis=0,
        tiled=True,
    ).reshape(slots, length + META)
    meta = received[:, length:length + 3].astype(jnp.int32)
    valid = meta[:, 2] == 1
    slot_bin = jnp.where(valid, meta[:, 0], -1)
    slot_class = jnp.where(valid, meta[:, 1], -1)
    select = (jnp.arange(bin_share, dtype=jnp.int32)[:, None] == slot_bin[None, :]).astype(
        jnp.bfloat16
    )
    matrices = jnp.stack(
        [
            moveout_matrix(nmo_coef[0, offset_index], band_shift[0, offset_index])
            for offset_index in range(nmo_coef.shape[1])
        ]
    )
    stacked = moveout_stack(received, slot_class[:, None], select, matrices, length)
    fold_share = fold[0].astype(jnp.float32)[:, None]
    filtered = filter_stack(stacked, bandpass_matrix(bandpass), fold_share)
    return filtered[None]


def solution(mesh):
    placed = (
        P(("line", "tile"), None),
        P(("line", "tile")),
        P(("line", "tile")),
        P(("line", "tile")),
        P("line", None, None, None),
        P("line", None, None),
        P(),
        P("line", "tile"),
    )
    return jax.shard_map(
        body, mesh=mesh, in_specs=placed, out_specs=P("line", "tile", None), check_vma=False
    )
```

```python
import jax
import jax.numpy as jnp
from jax import lax
from jax.sharding import PartitionSpec as P
from jax.experimental import pallas as pl
from jax.experimental.pallas import tpu as pltpu

META = 128


def moveout_matrix(coef_rows, shift_rows):
    taps_count = coef_rows.shape[0]
    groups = coef_rows.shape[1] // 128
    column = jnp.arange(128, dtype=jnp.int32).reshape(1, 1, 128)
    position = jnp.arange(256, dtype=jnp.int32).reshape(1, 256, 1)
    shifts = shift_rows.reshape(groups, 1, 128)
    weights = coef_rows.astype(jnp.float32).reshape(taps_count, groups, 1, 128)
    matrix = jnp.zeros((groups, 256, 128), jnp.float32)
    for tap_index in range(taps_count):
        matrix = matrix + jnp.where(
            position == column + shifts + tap_index, weights[tap_index], 0.0
        )
    return matrix.astype(jnp.bfloat16)


def split3(value):
    high = value.astype(jnp.bfloat16)
    rest = value - high.astype(jnp.float32)
    middle = rest.astype(jnp.bfloat16)
    low = (rest - middle.astype(jnp.float32)).astype(jnp.bfloat16)
    return high, middle, low


def moveout_kernel(rows_ref, class_ref, select_ref, matrix_ref, taps_ref, fold_ref, out_ref, stack_ref):
    step = pl.program_id(0)
    per_step = matrix_ref.shape[1]
    bins, length = out_ref.shape
    taps_count = taps_ref.shape[0]
    half = (taps_count - 1) // 2

    @pl.when(step == 0)
    def _():
        stack_ref[:, :128] = jnp.zeros((bins, 128), jnp.float32)
        stack_ref[:, length + 128:] = jnp.zeros((bins, 128), jnp.float32)

    slot_class = class_ref[...]
    select = select_ref[...]
    for inner in range(per_step):
        start = pl.multiple_of((step * per_step + inner) * 128, 128)
        window = rows_ref[:, pl.ds(start, 256)]
        lanes = start + lax.broadcasted_iota(jnp.int32, (1, 256), 1)
        window = jnp.where(lanes < length, window, jnp.zeros((), window.dtype))
        corrected = jnp.zeros((window.shape[0], 128), jnp.float32)
        for offset_index in range(matrix_ref.shape[0]):
            product = jnp.dot(
                window, matrix_ref[offset_index, inner], preferred_element_type=jnp.float32
            )
            corrected = corrected + jnp.where(slot_class == offset_index, product, 0.0)
        total = None
        for part in split3(corrected):
            piece = jnp.dot(select, part, preferred_element_type=jnp.float32)
            total = piece if total is None else total + piece
        stack_ref[:, pl.ds(start + 128, 128)] = total

    @pl.when(step == pl.num_programs(0) - 1)
    def _():
        width = length + 256
        for row in range(bins // 8):
            rows_now = stack_ref[row * 8:(row + 1) * 8, :]
            filtered = jnp.zeros((8, length), jnp.float32)
            for tap_index in range(taps_count):
                shift = (-(128 + tap_index - half)) % width
                moved = pltpu.roll(rows_now, shift, 1)[:, :length]
                filtered = filtered + taps_ref[tap_index:tap_index + 1, :] * moved
            out_ref[row * 8:(row + 1) * 8, :] = filtered / fold_ref[row * 8:(row + 1) * 8, :]


def moveout_stack(rows, slot_class, select, matrices, taps, fold_share, length):
    slot_count, width = rows.shape
    bins = select.shape[0]
    classes, groups = matrices.shape[0], matrices.shape[1]
    per_step = 4
    return pl.pallas_call(
        moveout_kernel,
        grid=(groups // per_step,),
        in_specs=[
            pl.BlockSpec((slot_count, width), lambda g: (0, 0)),
            pl.BlockSpec((slot_count, 1), lambda g: (0, 0)),
            pl.BlockSpec((bins, slot_count), lambda g: (0, 0)),
            pl.BlockSpec((classes, per_step, 256, 128), lambda g: (0, g, 0, 0)),
            pl.BlockSpec(taps.shape, lambda g: (0, 0)),
            pl.BlockSpec((bins, 1), lambda g: (0, 0)),
        ],
        out_specs=pl.BlockSpec((bins, length), lambda g: (0, 0)),
        out_shape=jax.ShapeDtypeStruct((bins, length), jnp.float32),
        scratch_shapes=[pltpu.VMEM((bins, length + 256), jnp.float32)],
    )(rows, slot_class, select, matrices, taps, fold_share)


def ranks(keys, key_count):
    onehot = (keys[:, None] == jnp.arange(key_count, dtype=jnp.int32)[None, :]).astype(jnp.int32)
    running = jnp.cumsum(onehot, 0)
    return jnp.sum(onehot * running, 1) - 1


def body(traces, trace_line, trace_bin, block_offset, nmo_coef, band_shift, bandpass, fold):
    line_count = lax.axis_size("line")
    tile_count = lax.axis_size("tile")
    trace_count, length = traces.shape
    block_rows = trace_count // block_offset.shape[0]
    bin_share = fold.shape[1]
    dest_count = line_count * tile_count
    capacity = 4
    slots = dest_count * capacity
    trace_class = jnp.repeat(block_offset, block_rows)
    trace_tile = trace_bin // bin_share
    dest = trace_line * tile_count + trace_tile
    slot_of_trace = dest * capacity + ranks(dest, dest_count)
    lane = jnp.arange(META, dtype=jnp.int32)[None, :]
    meta_block = jnp.where(
        lane == 0,
        (trace_bin % bin_share)[:, None],
        jnp.where(lane == 1, trace_class[:, None], jnp.where(lane == 2, 1, 0)),
    ).astype(jnp.bfloat16)
    extended = jnp.concatenate([traces, meta_block], 1)
    select = (
        jnp.arange(slots, dtype=jnp.int32)[:, None] == slot_of_trace[None, :]
    ).astype(jnp.bfloat16)
    send = jnp.dot(select, extended, preferred_element_type=jnp.float32).astype(jnp.bfloat16)
    received = lax.all_to_all(
        send.reshape(dest_count, capacity, length + META),
        ("line", "tile"),
        split_axis=0,
        concat_axis=0,
        tiled=True,
    ).reshape(slots, length + META)
    meta = received[:, length:length + 3].astype(jnp.int32)
    valid = meta[:, 2] == 1
    slot_bin = jnp.where(valid, meta[:, 0], -1)
    slot_class = jnp.where(valid, meta[:, 1], -1)
    select = (jnp.arange(bin_share, dtype=jnp.int32)[:, None] == slot_bin[None, :]).astype(
        jnp.bfloat16
    )
    matrices = jnp.stack(
        [
            moveout_matrix(nmo_coef[0, offset_index], band_shift[0, offset_index])
            for offset_index in range(nmo_coef.shape[1])
        ]
    )
    fold_share = fold[0].astype(jnp.float32)[:, None]
    filtered = moveout_stack(
        received, slot_class[:, None], select, matrices, bandpass, fold_share, length
    )
    return filtered[None]


def solution(mesh):
    placed = (
        P(("line", "tile"), None),
        P(("line", "tile")),
        P(("line", "tile")),
        P(("line", "tile")),
        P("line", None, None, None),
        P("line", None, None),
        P(),
        P("line", "tile"),
    )
    return jax.shard_map(
        body, mesh=mesh, in_specs=placed, out_specs=P("line", "tile", None), check_vma=False
    )
```

```python
import jax
import jax.numpy as jnp
from jax import lax
from jax.sharding import PartitionSpec as P
from jax.experimental import pallas as pl
from jax.experimental.pallas import tpu as pltpu

META = 128


def moveout_matrix(coef_rows, shift_rows):
    taps_count = coef_rows.shape[0]
    groups = coef_rows.shape[1] // 128
    column = jnp.arange(128, dtype=jnp.int32).reshape(1, 1, 128)
    position = jnp.arange(256, dtype=jnp.int32).reshape(1, 256, 1)
    shifts = shift_rows.reshape(groups, 1, 128)
    weights = coef_rows.astype(jnp.float32).reshape(taps_count, groups, 1, 128)
    matrix = jnp.zeros((groups, 256, 128), jnp.float32)
    for tap_index in range(taps_count):
        matrix = matrix + jnp.where(
            position == column + shifts + tap_index, weights[tap_index], 0.0
        )
    return matrix.astype(jnp.bfloat16)


def moveout_kernel(rows_ref, matrix_ref, taps_ref, fold_ref, out_ref, part_ref, stack_ref):
    step = pl.program_id(0)
    classes, per_step = matrix_ref.shape[0], matrix_ref.shape[1]
    bins, length = out_ref.shape
    slot_count, width = rows_ref.shape
    taps_count = taps_ref.shape[0]
    half = (taps_count - 1) // 2

    @pl.when(step == 0)
    def _():
        stack_ref[:, :128] = jnp.zeros((bins, 128), jnp.float32)
        stack_ref[:, length + 128:] = jnp.zeros((bins, 128), jnp.float32)
        meta = rows_ref[:, length:].astype(jnp.float32).T
        key = jnp.where(meta[2:3, :] == 1.0, meta[1:2, :] * bins + meta[0:1, :], -1.0)
        keys = lax.broadcasted_iota(jnp.int32, (classes * bins, slot_count), 0).astype(jnp.float32)
        select = (keys == key).astype(jnp.bfloat16)
        summed = jnp.dot(select, rows_ref[:, :length], preferred_element_type=jnp.float32)
        high = summed.astype(jnp.bfloat16)
        middle = (summed - high.astype(jnp.float32)).astype(jnp.bfloat16)
        for offset_index in range(classes):
            base = offset_index * 2 * bins
            part_ref[base:base + bins, :length] = high[offset_index * bins:(offset_index + 1) * bins]
            part_ref[base + bins:base + 2 * bins, :length] = middle[
                offset_index * bins:(offset_index + 1) * bins
            ]
        part_ref[:, length:] = jnp.zeros((classes * 2 * bins, width - length), jnp.bfloat16)

    for inner in range(per_step):
        start = pl.multiple_of((step * per_step + inner) * 128, 128)
        total = jnp.zeros((bins, 128), jnp.float32)
        for offset_index in range(classes):
            base = offset_index * 2 * bins
            window = part_ref[base:base + 2 * bins, pl.ds(start, 256)]
            product = jnp.dot(
                window, matrix_ref[offset_index, inner], preferred_element_type=jnp.float32
            )
            total = total + product[:bins] + product[bins:]
        stack_ref[:, pl.ds(start + 128, 128)] = total

    @pl.when(step == pl.num_programs(0) - 1)
    def _():
        span = length + 256
        for row in range(bins // 8):
            rows_now = stack_ref[row * 8:(row + 1) * 8, :]
            filtered = jnp.zeros((8, length), jnp.float32)
            for tap_index in range(taps_count):
                shift = (-(128 + tap_index - half)) % span
                moved = pltpu.roll(rows_now, shift, 1)[:, :length]
                filtered = filtered + taps_ref[tap_index:tap_index + 1, :] * moved
            out_ref[row * 8:(row + 1) * 8, :] = filtered / fold_ref[row * 8:(row + 1) * 8, :]


def moveout_stack(rows, matrices, taps, fold_share, length):
    slot_count, width = rows.shape
    bins = fold_share.shape[0]
    classes, groups = matrices.shape[0], matrices.shape[1]
    per_step = 4
    return pl.pallas_call(
        moveout_kernel,
        grid=(groups // per_step,),
        in_specs=[
            pl.BlockSpec((slot_count, width), lambda g: (0, 0)),
            pl.BlockSpec((classes, per_step, 256, 128), lambda g: (0, g, 0, 0)),
            pl.BlockSpec(taps.shape, lambda g: (0, 0)),
            pl.BlockSpec((bins, 1), lambda g: (0, 0)),
        ],
        out_specs=pl.BlockSpec((bins, length), lambda g: (0, 0)),
        out_shape=jax.ShapeDtypeStruct((bins, length), jnp.float32),
        scratch_shapes=[
            pltpu.VMEM((classes * 2 * bins, width), jnp.bfloat16),
            pltpu.VMEM((bins, length + 256), jnp.float32),
        ],
    )(rows, matrices, taps, fold_share)


def ranks(keys, key_count):
    onehot = (keys[:, None] == jnp.arange(key_count, dtype=jnp.int32)[None, :]).astype(jnp.int32)
    running = jnp.cumsum(onehot, 0)
    return jnp.sum(onehot * running, 1) - 1


def body(traces, trace_line, trace_bin, block_offset, nmo_coef, band_shift, bandpass, fold):
    line_count = lax.axis_size("line")
    tile_count = lax.axis_size("tile")
    trace_count, length = traces.shape
    block_rows = trace_count // block_offset.shape[0]
    bin_share = fold.shape[1]
    dest_count = line_count * tile_count
    capacity = 4
    slots = dest_count * capacity
    trace_class = jnp.repeat(block_offset, block_rows)
    trace_tile = trace_bin // bin_share
    dest = trace_line * tile_count + trace_tile
    slot_of_trace = dest * capacity + ranks(dest, dest_count)
    lane = jnp.arange(META, dtype=jnp.int32)[None, :]
    meta_block = jnp.where(
        lane == 0,
        (trace_bin % bin_share)[:, None],
        jnp.where(lane == 1, trace_class[:, None], jnp.where(lane == 2, 1, 0)),
    ).astype(jnp.bfloat16)
    extended = jnp.concatenate([traces, meta_block], 1)
    select = (
        jnp.arange(slots, dtype=jnp.int32)[:, None] == slot_of_trace[None, :]
    ).astype(jnp.bfloat16)
    send = jnp.dot(select, extended, preferred_element_type=jnp.float32).astype(jnp.bfloat16)
    received = lax.all_to_all(
        send.reshape(dest_count, capacity, length + META),
        ("line", "tile"),
        split_axis=0,
        concat_axis=0,
        tiled=True,
    ).reshape(slots, length + META)
    matrices = jnp.stack(
        [
            moveout_matrix(nmo_coef[0, offset_index], band_shift[0, offset_index])
            for offset_index in range(nmo_coef.shape[1])
        ]
    )
    fold_share = fold[0].astype(jnp.float32)[:, None]
    filtered = moveout_stack(received, matrices, bandpass, fold_share, length)
    return filtered[None]


def solution(mesh):
    placed = (
        P(("line", "tile"), None),
        P(("line", "tile")),
        P(("line", "tile")),
        P(("line", "tile")),
        P("line", None, None, None),
        P("line", None, None),
        P(),
        P("line", "tile"),
    )
    return jax.shard_map(
        body, mesh=mesh, in_specs=placed, out_specs=P("line", "tile", None), check_vma=False
    )
```

```python
import jax
import jax.numpy as jnp
from jax import lax
from jax.sharding import PartitionSpec as P
from jax.experimental import pallas as pl
from jax.experimental.pallas import tpu as pltpu

META = 128


def moveout_matrix(coef_rows, shift_rows):
    taps_count = coef_rows.shape[0]
    groups = coef_rows.shape[1] // 128
    column = jnp.arange(128, dtype=jnp.int32).reshape(1, 1, 128)
    position = jnp.arange(256, dtype=jnp.int32).reshape(1, 256, 1)
    shifts = shift_rows.reshape(groups, 1, 128)
    weights = coef_rows.astype(jnp.float32).reshape(taps_count, groups, 1, 128)
    matrix = jnp.zeros((groups, 256, 128), jnp.float32)
    for tap_index in range(taps_count):
        matrix = matrix + jnp.where(
            position == column + shifts + tap_index, weights[tap_index], 0.0
        )
    return matrix.astype(jnp.bfloat16)


def moveout_kernel(rows_ref, matrix_ref, taps_ref, fold_ref, out_ref, part_ref, stack_ref):
    step = pl.program_id(0)
    classes, per_step = matrix_ref.shape[0], matrix_ref.shape[1]
    bins, length = out_ref.shape
    sources, capacity, width = rows_ref.shape
    slot_count = sources * capacity
    taps_count = taps_ref.shape[0]
    half = (taps_count - 1) // 2

    @pl.when(step == 0)
    def _():
        stack_ref[:, :128] = jnp.zeros((bins, 128), jnp.float32)
        stack_ref[:, length + 128:] = jnp.zeros((bins, 128), jnp.float32)
        rows_all = rows_ref[...].reshape(slot_count, width)
        meta = rows_all[:, length:].astype(jnp.float32).T
        key = jnp.where(meta[2:3, :] == 1.0, meta[1:2, :] * bins + meta[0:1, :], -1.0)
        keys = lax.broadcasted_iota(jnp.int32, (classes * bins, slot_count), 0).astype(jnp.float32)
        select = (keys == key).astype(jnp.bfloat16)
        summed = jnp.dot(select, rows_all[:, :length], preferred_element_type=jnp.float32)
        high = summed.astype(jnp.bfloat16)
        middle = (summed - high.astype(jnp.float32)).astype(jnp.bfloat16)
        for offset_index in range(classes):
            base = offset_index * 2 * bins
            part_ref[base:base + bins, :length] = high[offset_index * bins:(offset_index + 1) * bins]
            part_ref[base + bins:base + 2 * bins, :length] = middle[
                offset_index * bins:(offset_index + 1) * bins
            ]
        part_ref[:, length:] = jnp.zeros((classes * 2 * bins, width - length), jnp.bfloat16)

    for inner in range(per_step):
        start = pl.multiple_of((step * per_step + inner) * 128, 128)
        total = jnp.zeros((bins, 128), jnp.float32)
        for offset_index in range(classes):
            base = offset_index * 2 * bins
            window = part_ref[base:base + 2 * bins, pl.ds(start, 256)]
            product = jnp.dot(
                window, matrix_ref[offset_index, inner], preferred_element_type=jnp.float32
            )
            total = total + product[:bins] + product[bins:]
        stack_ref[:, pl.ds(start + 128, 128)] = total

    @pl.when(step == pl.num_programs(0) - 1)
    def _():
        span = length + 256
        for row in range(bins // 8):
            rows_now = stack_ref[row * 8:(row + 1) * 8, :]
            filtered = jnp.zeros((8, length), jnp.float32)
            for tap_index in range(taps_count):
                shift = (-(128 + tap_index - half)) % span
                moved = pltpu.roll(rows_now, shift, 1)[:, :length]
                filtered = filtered + taps_ref[tap_index:tap_index + 1, :] * moved
            out_ref[row * 8:(row + 1) * 8, :] = filtered / fold_ref[row * 8:(row + 1) * 8, :]


def moveout_stack(rows, matrices, taps, fold_share, length):
    sources, capacity, width = rows.shape
    bins = fold_share.shape[0]
    classes, groups = matrices.shape[0], matrices.shape[1]
    per_step = 4
    return pl.pallas_call(
        moveout_kernel,
        grid=(groups // per_step,),
        in_specs=[
            pl.BlockSpec((sources, capacity, width), lambda g: (0, 0, 0)),
            pl.BlockSpec((classes, per_step, 256, 128), lambda g: (0, g, 0, 0)),
            pl.BlockSpec(taps.shape, lambda g: (0, 0)),
            pl.BlockSpec((bins, 1), lambda g: (0, 0)),
        ],
        out_specs=pl.BlockSpec((bins, length), lambda g: (0, 0)),
        out_shape=jax.ShapeDtypeStruct((bins, length), jnp.float32),
        scratch_shapes=[
            pltpu.VMEM((classes * 2 * bins, width), jnp.bfloat16),
            pltpu.VMEM((bins, length + 256), jnp.float32),
        ],
    )(rows, matrices, taps, fold_share)


def send_kernel(slot_ref, traces_ref, meta_ref, out_ref):
    dests, capacity, width = out_ref.shape
    trace_count, length = traces_ref.shape
    slots = dests * capacity
    wanted = lax.broadcasted_iota(jnp.int32, (slots, trace_count), 0)
    select = (wanted == slot_ref[...]).astype(jnp.bfloat16)
    rows = jnp.dot(select, traces_ref[...], preferred_element_type=jnp.float32)
    meta = jnp.dot(select, meta_ref[...], preferred_element_type=jnp.float32)
    out_ref[:, :, :length] = rows.astype(jnp.bfloat16).reshape(dests, capacity, length)
    out_ref[:, :, length:] = meta.astype(jnp.bfloat16).reshape(dests, capacity, width - length)


def build_send(slot_of_trace, traces, meta_block, dests, capacity):
    trace_count, length = traces.shape
    width = length + meta_block.shape[1]
    return pl.pallas_call(
        send_kernel,
        out_shape=jax.ShapeDtypeStruct((dests, capacity, width), jnp.bfloat16),
    )(slot_of_trace[None, :], traces, meta_block)


def ranks(keys, key_count):
    onehot = (keys[:, None] == jnp.arange(key_count, dtype=jnp.int32)[None, :]).astype(jnp.int32)
    running = jnp.cumsum(onehot, 0)
    return jnp.sum(onehot * running, 1) - 1


def body(traces, trace_line, trace_bin, block_offset, nmo_coef, band_shift, bandpass, fold):
    line_count = lax.axis_size("line")
    tile_count = lax.axis_size("tile")
    trace_count, length = traces.shape
    block_rows = trace_count // block_offset.shape[0]
    bin_share = fold.shape[1]
    dest_count = line_count * tile_count
    capacity = 4
    slots = dest_count * capacity
    trace_class = jnp.repeat(block_offset, block_rows)
    trace_tile = trace_bin // bin_share
    dest = trace_line * tile_count + trace_tile
    slot_of_trace = dest * capacity + ranks(dest, dest_count)
    lane = jnp.arange(META, dtype=jnp.int32)[None, :]
    meta_block = jnp.where(
        lane == 0,
        (trace_bin % bin_share)[:, None],
        jnp.where(lane == 1, trace_class[:, None], jnp.where(lane == 2, 1, 0)),
    ).astype(jnp.bfloat16)
    send = build_send(slot_of_trace, traces, meta_block, dest_count, capacity)
    received = lax.all_to_all(
        send,
        ("line", "tile"),
        split_axis=0,
        concat_axis=0,
        tiled=True,
    )
    matrices = jnp.stack(
        [
            moveout_matrix(nmo_coef[0, offset_index], band_shift[0, offset_index])
            for offset_index in range(nmo_coef.shape[1])
        ]
    )
    fold_share = fold[0].astype(jnp.float32)[:, None]
    filtered = moveout_stack(received, matrices, bandpass, fold_share, length)
    return filtered[None]


def solution(mesh):
    placed = (
        P(("line", "tile"), None),
        P(("line", "tile")),
        P(("line", "tile")),
        P(("line", "tile")),
        P("line", None, None, None),
        P("line", None, None),
        P(),
        P("line", "tile"),
    )
    return jax.shard_map(
        body, mesh=mesh, in_specs=placed, out_specs=P("line", "tile", None), check_vma=False
    )
```

```python
import functools

import jax
import jax.numpy as jnp
from jax import lax
from jax.sharding import PartitionSpec as P
from jax.experimental import pallas as pl
from jax.experimental.pallas import tpu as pltpu

META = 128


def moveout_matrix(coef_rows, shift_rows):
    taps_count = coef_rows.shape[0]
    groups = coef_rows.shape[1] // 128
    column = jnp.arange(128, dtype=jnp.int32).reshape(1, 1, 128)
    position = jnp.arange(256, dtype=jnp.int32).reshape(1, 256, 1)
    shifts = shift_rows.reshape(groups, 1, 128)
    weights = coef_rows.astype(jnp.float32).reshape(taps_count, groups, 1, 128)
    matrix = jnp.zeros((groups, 256, 128), jnp.float32)
    for tap_index in range(taps_count):
        matrix = matrix + jnp.where(
            position == column + shifts + tap_index, weights[tap_index], 0.0
        )
    return matrix.astype(jnp.bfloat16)


def moveout_kernel(rows_ref, matrix_ref, taps_ref, fold_ref, out_ref, part_ref, stack_ref):
    step = pl.program_id(0)
    classes, per_step = matrix_ref.shape[0], matrix_ref.shape[1]
    bins, length = out_ref.shape
    sources, capacity, width = rows_ref.shape
    slot_count = sources * capacity
    taps_count = taps_ref.shape[0]
    half = (taps_count - 1) // 2

    @pl.when(step == 0)
    def _():
        stack_ref[:, :128] = jnp.zeros((bins, 128), jnp.float32)
        stack_ref[:, length + 128:] = jnp.zeros((bins, 128), jnp.float32)
        rows_all = rows_ref[...].reshape(slot_count, width)
        meta = rows_all[:, length:].astype(jnp.float32).T
        key = jnp.where(meta[2:3, :] == 1.0, meta[1:2, :] * bins + meta[0:1, :], -1.0)
        keys = lax.broadcasted_iota(jnp.int32, (classes * bins, slot_count), 0).astype(jnp.float32)
        select = (keys == key).astype(jnp.bfloat16)
        summed = jnp.dot(select, rows_all[:, :length], preferred_element_type=jnp.float32)
        high = summed.astype(jnp.bfloat16)
        middle = (summed - high.astype(jnp.float32)).astype(jnp.bfloat16)
        for offset_index in range(classes):
            base = offset_index * 2 * bins
            part_ref[base:base + bins, :length] = high[offset_index * bins:(offset_index + 1) * bins]
            part_ref[base + bins:base + 2 * bins, :length] = middle[
                offset_index * bins:(offset_index + 1) * bins
            ]
        part_ref[:, length:] = jnp.zeros((classes * 2 * bins, width - length), jnp.bfloat16)

    for inner in range(per_step):
        start = pl.multiple_of((step * per_step + inner) * 128, 128)
        total = jnp.zeros((bins, 128), jnp.float32)
        for offset_index in range(classes):
            base = offset_index * 2 * bins
            window = part_ref[base:base + 2 * bins, pl.ds(start, 256)]
            product = jnp.dot(
                window, matrix_ref[offset_index, inner], preferred_element_type=jnp.float32
            )
            total = total + product[:bins] + product[bins:]
        stack_ref[:, pl.ds(start + 128, 128)] = total

    @pl.when(step == pl.num_programs(0) - 1)
    def _():
        span = length + 256
        for row in range(bins // 8):
            rows_now = stack_ref[row * 8:(row + 1) * 8, :]
            filtered = jnp.zeros((8, length), jnp.float32)
            for tap_index in range(taps_count):
                shift = (-(128 + tap_index - half)) % span
                moved = pltpu.roll(rows_now, shift, 1)[:, :length]
                filtered = filtered + taps_ref[tap_index:tap_index + 1, :] * moved
            out_ref[row * 8:(row + 1) * 8, :] = filtered / fold_ref[row * 8:(row + 1) * 8, :]


def moveout_stack(rows, matrices, taps, fold_share, length):
    sources, capacity, width = rows.shape
    bins = fold_share.shape[0]
    classes, groups = matrices.shape[0], matrices.shape[1]
    per_step = 4
    return pl.pallas_call(
        moveout_kernel,
        grid=(groups // per_step,),
        in_specs=[
            pl.BlockSpec((sources, capacity, width), lambda g: (0, 0, 0)),
            pl.BlockSpec((classes, per_step, 256, 128), lambda g: (0, g, 0, 0)),
            pl.BlockSpec(taps.shape, lambda g: (0, 0)),
            pl.BlockSpec((bins, 1), lambda g: (0, 0)),
        ],
        out_specs=pl.BlockSpec((bins, length), lambda g: (0, 0)),
        out_shape=jax.ShapeDtypeStruct((bins, length), jnp.float32),
        scratch_shapes=[
            pltpu.VMEM((classes * 2 * bins, width), jnp.bfloat16),
            pltpu.VMEM((bins, length + 256), jnp.float32),
        ],
    )(rows, matrices, taps, fold_share)


def send_kernel(ids_ref, traces_ref, out_ref, *, bins, tiles):
    dests, capacity, width = out_ref.shape
    trace_count, length = traces_ref.shape
    slots = dests * capacity
    ids = ids_ref[...]
    line_id, bin_id, class_id = ids[:, 0:1], ids[:, 1:2], ids[:, 2:3]
    dest = line_id * tiles + bin_id // bins
    onehot = (dest == lax.broadcasted_iota(jnp.int32, (trace_count, dests), 1)).astype(jnp.bfloat16)
    row = lax.broadcasted_iota(jnp.int32, (trace_count, trace_count), 0)
    col = lax.broadcasted_iota(jnp.int32, (trace_count, trace_count), 1)
    lower = (col <= row).astype(jnp.bfloat16)
    running = jnp.dot(lower, onehot, preferred_element_type=jnp.float32)
    rank = jnp.sum(running * onehot.astype(jnp.float32), axis=1, keepdims=True) - 1.0
    slot = dest.astype(jnp.float32) * capacity + rank
    wanted = lax.broadcasted_iota(jnp.int32, (trace_count, slots), 1).astype(jnp.float32)
    select = (wanted == slot).astype(jnp.float32).T.astype(jnp.bfloat16)
    lane = lax.broadcasted_iota(jnp.int32, (trace_count, width - length), 1)
    meta = jnp.where(
        lane == 0, bin_id % bins, jnp.where(lane == 1, class_id, jnp.where(lane == 2, 1, 0))
    ).astype(jnp.bfloat16)
    rows = jnp.dot(select, traces_ref[...], preferred_element_type=jnp.float32)
    meta_rows = jnp.dot(select, meta, preferred_element_type=jnp.float32)
    out_ref[:, :, :length] = rows.astype(jnp.bfloat16).reshape(dests, capacity, length)
    out_ref[:, :, length:] = meta_rows.astype(jnp.bfloat16).reshape(dests, capacity, width - length)


def build_send(ids, traces, dests, capacity, bins, tiles):
    trace_count, length = traces.shape
    width = length + META
    return pl.pallas_call(
        functools.partial(send_kernel, bins=bins, tiles=tiles),
        out_shape=jax.ShapeDtypeStruct((dests, capacity, width), jnp.bfloat16),
    )(ids, traces)


def body(traces, trace_line, trace_bin, block_offset, nmo_coef, band_shift, bandpass, fold):
    line_count = lax.axis_size("line")
    tile_count = lax.axis_size("tile")
    trace_count, length = traces.shape
    block_rows = trace_count // block_offset.shape[0]
    bin_share = fold.shape[1]
    dest_count = line_count * tile_count
    capacity = 4
    slots = dest_count * capacity
    trace_class = jnp.repeat(block_offset, block_rows)
    ids = jnp.stack([trace_line, trace_bin, trace_class], axis=1)
    send = build_send(ids, traces, dest_count, capacity, bin_share, tile_count)
    received = lax.all_to_all(
        send,
        ("line", "tile"),
        split_axis=0,
        concat_axis=0,
        tiled=True,
    )
    matrices = jnp.stack(
        [
            moveout_matrix(nmo_coef[0, offset_index], band_shift[0, offset_index])
            for offset_index in range(nmo_coef.shape[1])
        ]
    )
    fold_share = fold[0].astype(jnp.float32)[:, None]
    filtered = moveout_stack(received, matrices, bandpass, fold_share, length)
    return filtered[None]


def solution(mesh):
    placed = (
        P(("line", "tile"), None),
        P(("line", "tile")),
        P(("line", "tile")),
        P(("line", "tile")),
        P("line", None, None, None),
        P("line", None, None),
        P(),
        P("line", "tile"),
    )
    return jax.shard_map(
        body, mesh=mesh, in_specs=placed, out_specs=P("line", "tile", None), check_vma=False
    )
```

```python
import functools

import jax
import jax.numpy as jnp
from jax import lax
from jax.sharding import PartitionSpec as P
from jax.experimental import pallas as pl
from jax.experimental.pallas import tpu as pltpu

META = 128


def moveout_matrix(coef_rows, shift_rows):
    taps_count = coef_rows.shape[0]
    groups = coef_rows.shape[1] // 128
    column = jnp.arange(128, dtype=jnp.int32).reshape(1, 1, 128)
    position = jnp.arange(256, dtype=jnp.int32).reshape(1, 256, 1)
    shifts = shift_rows.reshape(groups, 1, 128)
    weights = coef_rows.astype(jnp.float32).reshape(taps_count, groups, 1, 128)
    matrix = jnp.zeros((groups, 256, 128), jnp.float32)
    for tap_index in range(taps_count):
        matrix = matrix + jnp.where(
            position == column + shifts + tap_index, weights[tap_index], 0.0
        )
    return matrix.astype(jnp.bfloat16)


def moveout_kernel(rows_ref, matrix_ref, taps_ref, fold_ref, out_ref, part_ref, stack_ref):
    step = pl.program_id(0)
    classes, per_step = matrix_ref.shape[0], matrix_ref.shape[1]
    bins, length = out_ref.shape
    sources, capacity, width = rows_ref.shape
    slot_count = sources * capacity
    taps_count = taps_ref.shape[0]
    half = (taps_count - 1) // 2

    @pl.when(step == 0)
    def _():
        stack_ref[:, :128] = jnp.zeros((bins, 128), jnp.float32)
        stack_ref[:, length + 128:] = jnp.zeros((bins, 128), jnp.float32)
        rows_all = rows_ref[...].reshape(slot_count, width)
        meta = rows_all[:, length:].astype(jnp.float32).T
        key = jnp.where(meta[2:3, :] == 1.0, meta[1:2, :] * bins + meta[0:1, :], -1.0)
        keys = lax.broadcasted_iota(jnp.int32, (classes * bins, slot_count), 0).astype(jnp.float32)
        select = (keys == key).astype(jnp.bfloat16)
        summed = jnp.dot(select, rows_all[:, :length], preferred_element_type=jnp.float32)
        high = summed.astype(jnp.bfloat16)
        middle = (summed - high.astype(jnp.float32)).astype(jnp.bfloat16)
        for offset_index in range(classes):
            base = offset_index * 2 * bins
            part_ref[base:base + bins, :length] = high[offset_index * bins:(offset_index + 1) * bins]
            part_ref[base + bins:base + 2 * bins, :length] = middle[
                offset_index * bins:(offset_index + 1) * bins
            ]
        part_ref[:, length:] = jnp.zeros((classes * 2 * bins, width - length), jnp.bfloat16)

    for inner in range(per_step):
        start = pl.multiple_of((step * per_step + inner) * 128, 128)
        total = jnp.zeros((bins, 128), jnp.float32)
        for offset_index in range(classes):
            base = offset_index * 2 * bins
            window = part_ref[base:base + 2 * bins, pl.ds(start, 256)]
            product = jnp.dot(
                window, matrix_ref[offset_index, inner], preferred_element_type=jnp.float32
            )
            total = total + product[:bins] + product[bins:]
        stack_ref[:, pl.ds(start + 128, 128)] = total

    @pl.when(step == pl.num_programs(0) - 1)
    def _():
        span = length + 256
        for row in range(bins // 8):
            rows_now = stack_ref[row * 8:(row + 1) * 8, :]
            filtered = jnp.zeros((8, length), jnp.float32)
            for tap_index in range(taps_count):
                shift = (-(128 + tap_index - half)) % span
                moved = pltpu.roll(rows_now, shift, 1)[:, :length]
                filtered = filtered + taps_ref[tap_index:tap_index + 1, :] * moved
            out_ref[row * 8:(row + 1) * 8, :] = filtered / fold_ref[row * 8:(row + 1) * 8, :]


def moveout_stack(rows, matrices, taps, fold_share, length):
    sources, capacity, width = rows.shape
    bins = fold_share.shape[0]
    classes, groups = matrices.shape[0], matrices.shape[1]
    per_step = 4
    return pl.pallas_call(
        moveout_kernel,
        grid=(groups // per_step,),
        in_specs=[
            pl.BlockSpec((sources, capacity, width), lambda g: (0, 0, 0)),
            pl.BlockSpec((classes, per_step, 256, 128), lambda g: (0, g, 0, 0)),
            pl.BlockSpec(taps.shape, lambda g: (0, 0)),
            pl.BlockSpec((bins, 1), lambda g: (0, 0)),
        ],
        out_specs=pl.BlockSpec((bins, length), lambda g: (0, 0)),
        out_shape=jax.ShapeDtypeStruct((bins, length), jnp.float32),
        scratch_shapes=[
            pltpu.VMEM((classes * 2 * bins, width), jnp.bfloat16),
            pltpu.VMEM((bins, length + 256), jnp.float32),
        ],
    )(rows, matrices, taps, fold_share)


def send_kernel(line_ref, bin_ref, offset_ref, traces_ref, out_ref, *, bins, tiles):
    dests, capacity, width = out_ref.shape
    trace_count, length = traces_ref.shape
    slots = dests * capacity
    block = trace_count // offset_ref.shape[0]
    line_id = line_ref[...].reshape(trace_count, 1)
    bin_id = bin_ref[...].reshape(trace_count, 1)
    trace_index = lax.broadcasted_iota(jnp.int32, (trace_count, 1), 0)
    class_id = jnp.zeros((trace_count, 1), jnp.int32)
    for block_index in range(offset_ref.shape[0]):
        class_id = jnp.where(trace_index // block == block_index, offset_ref[block_index], class_id)
    dest = line_id * tiles + bin_id // bins
    onehot = (dest == lax.broadcasted_iota(jnp.int32, (trace_count, dests), 1)).astype(jnp.bfloat16)
    row = lax.broadcasted_iota(jnp.int32, (trace_count, trace_count), 0)
    col = lax.broadcasted_iota(jnp.int32, (trace_count, trace_count), 1)
    lower = (col <= row).astype(jnp.bfloat16)
    running = jnp.dot(lower, onehot, preferred_element_type=jnp.float32)
    rank = jnp.sum(running * onehot.astype(jnp.float32), axis=1, keepdims=True) - 1.0
    slot = dest.astype(jnp.float32) * capacity + rank
    wanted = lax.broadcasted_iota(jnp.int32, (trace_count, slots), 1).astype(jnp.float32)
    select = (wanted == slot).astype(jnp.float32).T.astype(jnp.bfloat16)
    lane = lax.broadcasted_iota(jnp.int32, (trace_count, width - length), 1)
    meta = jnp.where(
        lane == 0, bin_id % bins, jnp.where(lane == 1, class_id, jnp.where(lane == 2, 1, 0))
    ).astype(jnp.bfloat16)
    rows = jnp.dot(select, traces_ref[...], preferred_element_type=jnp.float32)
    meta_rows = jnp.dot(select, meta, preferred_element_type=jnp.float32)
    out_ref[:, :, :length] = rows.astype(jnp.bfloat16).reshape(dests, capacity, length)
    out_ref[:, :, length:] = meta_rows.astype(jnp.bfloat16).reshape(dests, capacity, width - length)


def build_send(trace_line, trace_bin, block_offset, traces, dests, capacity, bins, tiles):
    trace_count, length = traces.shape
    width = length + META
    in_vmem = pl.BlockSpec(memory_space=pltpu.VMEM)
    return pl.pallas_call(
        functools.partial(send_kernel, bins=bins, tiles=tiles),
        in_specs=[in_vmem, in_vmem, pl.BlockSpec(memory_space=pltpu.SMEM), in_vmem],
        out_shape=jax.ShapeDtypeStruct((dests, capacity, width), jnp.bfloat16),
    )(trace_line, trace_bin, block_offset, traces)


def body(traces, trace_line, trace_bin, block_offset, nmo_coef, band_shift, bandpass, fold):
    line_count = lax.axis_size("line")
    tile_count = lax.axis_size("tile")
    trace_count, length = traces.shape
    block_rows = trace_count // block_offset.shape[0]
    bin_share = fold.shape[1]
    dest_count = line_count * tile_count
    capacity = 4
    slots = dest_count * capacity
    send = build_send(
        trace_line, trace_bin, block_offset, traces, dest_count, capacity, bin_share, tile_count
    )
    received = lax.all_to_all(
        send,
        ("line", "tile"),
        split_axis=0,
        concat_axis=0,
        tiled=True,
    )
    matrices = jnp.stack(
        [
            moveout_matrix(nmo_coef[0, offset_index], band_shift[0, offset_index])
            for offset_index in range(nmo_coef.shape[1])
        ]
    )
    fold_share = fold[0].astype(jnp.float32)[:, None]
    filtered = moveout_stack(received, matrices, bandpass, fold_share, length)
    return filtered[None]


def solution(mesh):
    placed = (
        P(("line", "tile"), None),
        P(("line", "tile")),
        P(("line", "tile")),
        P(("line", "tile")),
        P("line", None, None, None),
        P("line", None, None),
        P(),
        P("line", "tile"),
    )
    return jax.shard_map(
        body, mesh=mesh, in_specs=placed, out_specs=P("line", "tile", None), check_vma=False
    )
```

```python
import functools

import jax
import jax.numpy as jnp
from jax import lax
from jax.sharding import PartitionSpec as P
from jax.experimental import pallas as pl
from jax.experimental.pallas import tpu as pltpu

META = 128
PAD = 16


def moveout_matrix(coef_rows, shift_rows):
    taps_count = coef_rows.shape[0]
    groups = coef_rows.shape[1] // 128
    column = jnp.arange(128, dtype=jnp.int32).reshape(1, 1, 128)
    position = jnp.arange(256, dtype=jnp.int32).reshape(1, 256, 1)
    shifts = shift_rows.reshape(groups, 1, 128)
    weights = coef_rows.astype(jnp.float32).reshape(taps_count, groups, 1, 128)
    matrix = jnp.zeros((groups, 256, 128), jnp.float32)
    for tap_index in range(taps_count):
        matrix = matrix + jnp.where(
            position == column + shifts + tap_index, weights[tap_index], 0.0
        )
    return matrix.astype(jnp.bfloat16)


def moveout_kernel(rows_ref, matrix_ref, taps_ref, fold_ref, out_ref, part_ref, stack_ref):
    step = pl.program_id(0)
    classes, per_step = matrix_ref.shape[0], matrix_ref.shape[1]
    bins, length = out_ref.shape
    sources, capacity, width = rows_ref.shape
    slot_count = sources * capacity

    @pl.when(step == 0)
    def _():
        stack_ref[:, :128] = jnp.zeros((bins, 128), jnp.float32)
        stack_ref[:, length + 128:] = jnp.zeros((bins, 128), jnp.float32)
        rows_all = rows_ref[...].reshape(slot_count, width)
        meta = rows_all[:, length:].astype(jnp.float32).T
        key = jnp.where(meta[2:3, :] == 1.0, meta[1:2, :] * bins + meta[0:1, :], -1.0)
        keys = lax.broadcasted_iota(jnp.int32, (classes * bins, slot_count), 0).astype(jnp.float32)
        select = (keys == key).astype(jnp.bfloat16)
        summed = jnp.dot(select, rows_all[:, :length], preferred_element_type=jnp.float32)
        high = summed.astype(jnp.bfloat16)
        middle = (summed - high.astype(jnp.float32)).astype(jnp.bfloat16)
        for offset_index in range(classes):
            base = offset_index * 2 * bins
            part_ref[base:base + bins, :length] = high[offset_index * bins:(offset_index + 1) * bins]
            part_ref[base + bins:base + 2 * bins, :length] = middle[
                offset_index * bins:(offset_index + 1) * bins
            ]
        part_ref[:, length:] = jnp.zeros((classes * 2 * bins, width - length), jnp.bfloat16)

    for inner in range(per_step):
        start = pl.multiple_of((step * per_step + inner) * 128, 128)
        total = jnp.zeros((bins, 128), jnp.float32)
        for offset_index in range(classes):
            base = offset_index * 2 * bins
            window = part_ref[base:base + 2 * bins, pl.ds(start, 256)]
            product = jnp.dot(
                window, matrix_ref[offset_index, inner], preferred_element_type=jnp.float32
            )
            total = total + product[:bins] + product[bins:]
        stack_ref[:, pl.ds(start + 128, 128)] = total

    @pl.when(step == pl.num_programs(0) - 1)
    def _():
        for group in range(length // 128):
            start = group * 128
            window = stack_ref[:, start + 128 - PAD:start + 384 - PAD]
            filtered = jnp.dot(
                window,
                taps_ref[group],
                precision=lax.Precision.HIGHEST,
                preferred_element_type=jnp.float32,
            )
            out_ref[:, start:start + 128] = filtered / fold_ref[...]


def moveout_stack(rows, matrices, taps, fold_share, length):
    sources, capacity, width = rows.shape
    bins = fold_share.shape[0]
    classes, groups = matrices.shape[0], matrices.shape[1]
    per_step = 4
    return pl.pallas_call(
        moveout_kernel,
        grid=(groups // per_step,),
        in_specs=[
            pl.BlockSpec((sources, capacity, width), lambda g: (0, 0, 0)),
            pl.BlockSpec((classes, per_step, 256, 128), lambda g: (0, g, 0, 0)),
            pl.BlockSpec(taps.shape, lambda g: (0, 0, 0)),
            pl.BlockSpec((bins, 1), lambda g: (0, 0)),
        ],
        out_specs=pl.BlockSpec((bins, length), lambda g: (0, 0)),
        out_shape=jax.ShapeDtypeStruct((bins, length), jnp.float32),
        scratch_shapes=[
            pltpu.VMEM((classes * 2 * bins, width), jnp.bfloat16),
            pltpu.VMEM((bins, length + 256), jnp.float32),
        ],
    )(rows, matrices, taps, fold_share)


def filter_matrix(taps):
    taps_count = taps.shape[0]
    groups = taps.shape[1] // 128
    half = (taps_count - 1) // 2
    column = jnp.arange(128, dtype=jnp.int32).reshape(1, 1, 128)
    position = jnp.arange(256, dtype=jnp.int32).reshape(1, 256, 1)
    weights = taps.reshape(taps_count, groups, 1, 128)
    matrix = jnp.zeros((groups, 256, 128), jnp.float32)
    for tap_index in range(taps_count):
        matrix = matrix + jnp.where(
            position == column + PAD + tap_index - half, weights[tap_index], 0.0
        )
    return matrix


def send_kernel(line_ref, bin_ref, offset_ref, traces_ref, out_ref, *, bins, tiles):
    dests, capacity, width = out_ref.shape
    trace_count, length = traces_ref.shape
    slots = dests * capacity
    block = trace_count // offset_ref.shape[0]
    line_id = line_ref[...].reshape(trace_count, 1)
    bin_id = bin_ref[...].reshape(trace_count, 1)
    trace_index = lax.broadcasted_iota(jnp.int32, (trace_count, 1), 0)
    class_id = jnp.zeros((trace_count, 1), jnp.int32)
    for block_index in range(offset_ref.shape[0]):
        class_id = jnp.where(trace_index // block == block_index, offset_ref[block_index], class_id)
    dest = line_id * tiles + bin_id // bins
    onehot = (dest == lax.broadcasted_iota(jnp.int32, (trace_count, dests), 1)).astype(jnp.bfloat16)
    row = lax.broadcasted_iota(jnp.int32, (trace_count, trace_count), 0)
    col = lax.broadcasted_iota(jnp.int32, (trace_count, trace_count), 1)
    lower = (col <= row).astype(jnp.bfloat16)
    running = jnp.dot(lower, onehot, preferred_element_type=jnp.float32)
    rank = jnp.sum(running * onehot.astype(jnp.float32), axis=1, keepdims=True) - 1.0
    slot = dest.astype(jnp.float32) * capacity + rank
    wanted = lax.broadcasted_iota(jnp.int32, (trace_count, slots), 1).astype(jnp.float32)
    select = (wanted == slot).astype(jnp.float32).T.astype(jnp.bfloat16)
    lane = lax.broadcasted_iota(jnp.int32, (trace_count, width - length), 1)
    meta = jnp.where(
        lane == 0, bin_id % bins, jnp.where(lane == 1, class_id, jnp.where(lane == 2, 1, 0))
    ).astype(jnp.bfloat16)
    rows = jnp.dot(select, traces_ref[...], preferred_element_type=jnp.float32)
    meta_rows = jnp.dot(select, meta, preferred_element_type=jnp.float32)
    out_ref[:, :, :length] = rows.astype(jnp.bfloat16).reshape(dests, capacity, length)
    out_ref[:, :, length:] = meta_rows.astype(jnp.bfloat16).reshape(dests, capacity, width - length)


def build_send(trace_line, trace_bin, block_offset, traces, dests, capacity, bins, tiles):
    trace_count, length = traces.shape
    width = length + META
    in_vmem = pl.BlockSpec(memory_space=pltpu.VMEM)
    return pl.pallas_call(
        functools.partial(send_kernel, bins=bins, tiles=tiles),
        in_specs=[in_vmem, in_vmem, pl.BlockSpec(memory_space=pltpu.SMEM), in_vmem],
        out_shape=jax.ShapeDtypeStruct((dests, capacity, width), jnp.bfloat16),
    )(trace_line, trace_bin, block_offset, traces)


def body(traces, trace_line, trace_bin, block_offset, nmo_coef, band_shift, bandpass, fold):
    line_count = lax.axis_size("line")
    tile_count = lax.axis_size("tile")
    trace_count, length = traces.shape
    block_rows = trace_count // block_offset.shape[0]
    bin_share = fold.shape[1]
    dest_count = line_count * tile_count
    capacity = 4
    slots = dest_count * capacity
    send = build_send(
        trace_line, trace_bin, block_offset, traces, dest_count, capacity, bin_share, tile_count
    )
    received = lax.all_to_all(
        send,
        ("line", "tile"),
        split_axis=0,
        concat_axis=0,
        tiled=True,
    )
    matrices = jnp.stack(
        [
            moveout_matrix(nmo_coef[0, offset_index], band_shift[0, offset_index])
            for offset_index in range(nmo_coef.shape[1])
        ]
    )
    fold_share = fold[0].astype(jnp.float32)[:, None]
    filtered = moveout_stack(received, matrices, filter_matrix(bandpass), fold_share, length)
    return filtered[None]


def solution(mesh):
    placed = (
        P(("line", "tile"), None),
        P(("line", "tile")),
        P(("line", "tile")),
        P(("line", "tile")),
        P("line", None, None, None),
        P("line", None, None),
        P(),
        P("line", "tile"),
    )
    return jax.shard_map(
        body, mesh=mesh, in_specs=placed, out_specs=P("line", "tile", None), check_vma=False
    )
```

```python
import functools

import jax
import jax.numpy as jnp
from jax import lax
from jax.sharding import PartitionSpec as P
from jax.experimental import pallas as pl
from jax.experimental.pallas import tpu as pltpu

META = 128
PAD = 16


def moveout_matrix(coef_rows, shift_rows):
    taps_count = coef_rows.shape[0]
    groups = coef_rows.shape[1] // 128
    column = jnp.arange(128, dtype=jnp.int32).reshape(1, 1, 128)
    position = jnp.arange(256, dtype=jnp.int32).reshape(1, 256, 1)
    shifts = shift_rows.reshape(groups, 1, 128)
    weights = coef_rows.astype(jnp.float32).reshape(taps_count, groups, 1, 128)
    matrix = jnp.zeros((groups, 256, 128), jnp.float32)
    for tap_index in range(taps_count):
        matrix = matrix + jnp.where(
            position == column + shifts + tap_index, weights[tap_index], 0.0
        )
    return matrix.astype(jnp.bfloat16)


def moveout_kernel(rows_ref, matrix_ref, taps_ref, fold_ref, out_ref, part_ref, stack_ref):
    step = pl.program_id(0)
    classes, per_step = matrix_ref.shape[0], matrix_ref.shape[1]
    bins, length = out_ref.shape
    sources, capacity, width = rows_ref.shape
    slot_count = sources * capacity

    @pl.when(step == 0)
    def _():
        stack_ref[:, :128] = jnp.zeros((bins, 128), jnp.float32)
        stack_ref[:, length + 128:] = jnp.zeros((bins, 128), jnp.float32)
        rows_all = rows_ref[...].reshape(slot_count, width)
        meta = rows_all[:, length:].astype(jnp.float32).T
        key = jnp.where(meta[2:3, :] == 1.0, meta[1:2, :] * bins + meta[0:1, :], -1.0)
        keys = lax.broadcasted_iota(jnp.int32, (classes * bins, slot_count), 0).astype(jnp.float32)
        select = (keys == key).astype(jnp.bfloat16)
        summed = jnp.dot(select, rows_all[:, :length], preferred_element_type=jnp.float32)
        high = summed.astype(jnp.bfloat16)
        middle = (summed - high.astype(jnp.float32)).astype(jnp.bfloat16)
        for offset_index in range(classes):
            base = offset_index * 2 * bins
            part_ref[base:base + bins, :length] = high[offset_index * bins:(offset_index + 1) * bins]
            part_ref[base + bins:base + 2 * bins, :length] = middle[
                offset_index * bins:(offset_index + 1) * bins
            ]
        part_ref[:, length:] = jnp.zeros((classes * 2 * bins, width - length), jnp.bfloat16)

    for inner in range(per_step):
        start = pl.multiple_of((step * per_step + inner) * 128, 128)
        total = jnp.zeros((bins, 128), jnp.float32)
        for offset_index in range(classes):
            base = offset_index * 2 * bins
            window = part_ref[base:base + 2 * bins, pl.ds(start, 256)]
            product = jnp.dot(
                window, matrix_ref[offset_index, inner], preferred_element_type=jnp.float32
            )
            total = total + product[:bins] + product[bins:]
        stack_ref[:, pl.ds(start + 128, 128)] = total

    @pl.when(step == pl.num_programs(0) - 1)
    def _():
        for group in range(length // 128):
            start = group * 128
            window = stack_ref[:, start + 128 - PAD:start + 384 - PAD]
            filtered = jnp.dot(
                window,
                taps_ref[group],
                precision=lax.Precision.HIGHEST,
                preferred_element_type=jnp.float32,
            )
            out_ref[:, start:start + 128] = filtered / fold_ref[...]


def moveout_stack(rows, matrices, taps, fold_share, length):
    sources, capacity, width = rows.shape
    bins = fold_share.shape[0]
    classes, groups = matrices.shape[0], matrices.shape[1]
    per_step = 4
    return pl.pallas_call(
        moveout_kernel,
        grid=(groups // per_step,),
        in_specs=[
            pl.BlockSpec((sources, capacity, width), lambda g: (0, 0, 0)),
            pl.BlockSpec((classes, per_step, 256, 128), lambda g: (0, g, 0, 0)),
            pl.BlockSpec(taps.shape, lambda g: (0, 0, 0)),
            pl.BlockSpec((bins, 1), lambda g: (0, 0)),
        ],
        out_specs=pl.BlockSpec((bins, length), lambda g: (0, 0)),
        out_shape=jax.ShapeDtypeStruct((bins, length), jnp.float32),
        scratch_shapes=[
            pltpu.VMEM((classes * 2 * bins, width), jnp.bfloat16),
            pltpu.VMEM((bins, length + 256), jnp.float32),
        ],
    )(rows, matrices, taps, fold_share)


def filter_matrix(taps):
    taps_count, length = taps.shape
    groups = length // 128
    half = (taps_count - 1) // 2
    span = 384
    placed = taps.T.reshape(groups, 128, taps_count)
    lead = PAD - half
    placed = jnp.pad(placed, ((0, 0), (0, 0), (lead, span - taps_count - lead)))
    flat = placed.reshape(groups, 128 * span)[:, : 128 * (span - 1)]
    skewed = flat.reshape(groups, 128, span - 1)[:, :, :256]
    return jnp.transpose(skewed, (0, 2, 1))


def send_kernel(line_ref, bin_ref, offset_ref, traces_ref, out_ref, *, bins, tiles):
    dests, capacity, width = out_ref.shape
    trace_count, length = traces_ref.shape
    slots = dests * capacity
    block = trace_count // offset_ref.shape[0]
    line_id = line_ref[...].reshape(trace_count, 1)
    bin_id = bin_ref[...].reshape(trace_count, 1)
    trace_index = lax.broadcasted_iota(jnp.int32, (trace_count, 1), 0)
    class_id = jnp.zeros((trace_count, 1), jnp.int32)
    for block_index in range(offset_ref.shape[0]):
        class_id = jnp.where(trace_index // block == block_index, offset_ref[block_index], class_id)
    dest = line_id * tiles + bin_id // bins
    onehot = (dest == lax.broadcasted_iota(jnp.int32, (trace_count, dests), 1)).astype(jnp.bfloat16)
    row = lax.broadcasted_iota(jnp.int32, (trace_count, trace_count), 0)
    col = lax.broadcasted_iota(jnp.int32, (trace_count, trace_count), 1)
    lower = (col <= row).astype(jnp.bfloat16)
    running = jnp.dot(lower, onehot, preferred_element_type=jnp.float32)
    rank = jnp.sum(running * onehot.astype(jnp.float32), axis=1, keepdims=True) - 1.0
    slot = dest.astype(jnp.float32) * capacity + rank
    wanted = lax.broadcasted_iota(jnp.int32, (trace_count, slots), 1).astype(jnp.float32)
    select = (wanted == slot).astype(jnp.float32).T.astype(jnp.bfloat16)
    lane = lax.broadcasted_iota(jnp.int32, (trace_count, width - length), 1)
    meta = jnp.where(
        lane == 0, bin_id % bins, jnp.where(lane == 1, class_id, jnp.where(lane == 2, 1, 0))
    ).astype(jnp.bfloat16)
    rows = jnp.dot(select, traces_ref[...], preferred_element_type=jnp.float32)
    meta_rows = jnp.dot(select, meta, preferred_element_type=jnp.float32)
    out_ref[:, :, :length] = rows.astype(jnp.bfloat16).reshape(dests, capacity, length)
    out_ref[:, :, length:] = meta_rows.astype(jnp.bfloat16).reshape(dests, capacity, width - length)


def build_send(trace_line, trace_bin, block_offset, traces, dests, capacity, bins, tiles):
    trace_count, length = traces.shape
    width = length + META
    in_vmem = pl.BlockSpec(memory_space=pltpu.VMEM)
    return pl.pallas_call(
        functools.partial(send_kernel, bins=bins, tiles=tiles),
        in_specs=[in_vmem, in_vmem, pl.BlockSpec(memory_space=pltpu.SMEM), in_vmem],
        out_shape=jax.ShapeDtypeStruct((dests, capacity, width), jnp.bfloat16),
    )(trace_line, trace_bin, block_offset, traces)


def body(traces, trace_line, trace_bin, block_offset, nmo_coef, band_shift, bandpass, fold):
    line_count = lax.axis_size("line")
    tile_count = lax.axis_size("tile")
    trace_count, length = traces.shape
    block_rows = trace_count // block_offset.shape[0]
    bin_share = fold.shape[1]
    dest_count = line_count * tile_count
    capacity = 4
    slots = dest_count * capacity
    send = build_send(
        trace_line, trace_bin, block_offset, traces, dest_count, capacity, bin_share, tile_count
    )
    received = lax.all_to_all(
        send,
        ("line", "tile"),
        split_axis=0,
        concat_axis=0,
        tiled=True,
    )
    matrices = jnp.stack(
        [
            moveout_matrix(nmo_coef[0, offset_index], band_shift[0, offset_index])
            for offset_index in range(nmo_coef.shape[1])
        ]
    )
    fold_share = fold[0].astype(jnp.float32)[:, None]
    filtered = moveout_stack(received, matrices, filter_matrix(bandpass), fold_share, length)
    return filtered[None]


def solution(mesh):
    placed = (
        P(("line", "tile"), None),
        P(("line", "tile")),
        P(("line", "tile")),
        P(("line", "tile")),
        P("line", None, None, None),
        P("line", None, None),
        P(),
        P("line", "tile"),
    )
    return jax.shard_map(
        body, mesh=mesh, in_specs=placed, out_specs=P("line", "tile", None), check_vma=False
    )
```

```python
import functools

import jax
import jax.numpy as jnp
from jax import lax
from jax.sharding import PartitionSpec as P
from jax.experimental import pallas as pl
from jax.experimental.pallas import tpu as pltpu

META = 128
PAD = 16


def moveout_matrix(coef_rows, shift_rows):
    taps_count = coef_rows.shape[0]
    groups = coef_rows.shape[1] // 128
    column = jnp.arange(128, dtype=jnp.int32).reshape(1, 1, 128)
    position = jnp.arange(256, dtype=jnp.int32).reshape(1, 256, 1)
    shifts = shift_rows.reshape(groups, 1, 128)
    weights = coef_rows.astype(jnp.float32).reshape(taps_count, groups, 1, 128)
    matrix = jnp.zeros((groups, 256, 128), jnp.float32)
    for tap_index in range(taps_count):
        matrix = matrix + jnp.where(
            position == column + shifts + tap_index, weights[tap_index], 0.0
        )
    return matrix.astype(jnp.bfloat16)


def moveout_kernel(rows_ref, matrix_ref, taps_ref, fold_ref, out_ref, part_ref, stack_ref):
    step = pl.program_id(0)
    last = pl.num_programs(0) - 1
    classes, per_step = matrix_ref.shape[0], matrix_ref.shape[1]
    bins, length = stack_ref.shape[0], stack_ref.shape[1] - 256
    sources, capacity, width = rows_ref.shape
    slot_count = sources * capacity

    @pl.when(step == 0)
    def _():
        stack_ref[:, :128] = jnp.zeros((bins, 128), jnp.float32)
        stack_ref[:, length + 128:] = jnp.zeros((bins, 128), jnp.float32)
        rows_all = rows_ref[...].reshape(slot_count, width)
        meta = rows_all[:, length:].astype(jnp.float32).T
        key = jnp.where(meta[2:3, :] == 1.0, meta[1:2, :] * bins + meta[0:1, :], -1.0)
        keys = lax.broadcasted_iota(jnp.int32, (classes * bins, slot_count), 0).astype(jnp.float32)
        select = (keys == key).astype(jnp.bfloat16)
        summed = jnp.dot(select, rows_all[:, :length], preferred_element_type=jnp.float32)
        high = summed.astype(jnp.bfloat16)
        middle = (summed - high.astype(jnp.float32)).astype(jnp.bfloat16)
        for offset_index in range(classes):
            base = offset_index * 2 * bins
            part_ref[base:base + bins, :length] = high[offset_index * bins:(offset_index + 1) * bins]
            part_ref[base + bins:base + 2 * bins, :length] = middle[
                offset_index * bins:(offset_index + 1) * bins
            ]
        part_ref[:, length:] = jnp.zeros((classes * 2 * bins, width - length), jnp.bfloat16)

    @pl.when(step < last)
    def _():
        for inner in range(per_step):
            start = pl.multiple_of((step * per_step + inner) * 128, 128)
            total = jnp.zeros((bins, 128), jnp.float32)
            for offset_index in range(classes):
                base = offset_index * 2 * bins
                window = part_ref[base:base + 2 * bins, pl.ds(start, 256)]
                product = jnp.dot(
                    window, matrix_ref[offset_index, inner], preferred_element_type=jnp.float32
                )
                total = total + product[:bins] + product[bins:]
            stack_ref[:, pl.ds(start + 128, 128)] = total

    @pl.when(step > 0)
    def _():
        for inner in range(per_step):
            start = pl.multiple_of(((step - 1) * per_step + inner) * 128, 128)
            window = stack_ref[:, pl.ds(start, 384)][:, 128 - PAD:384 - PAD]
            filtered = jnp.dot(
                window,
                taps_ref[inner],
                precision=lax.Precision.HIGHEST,
                preferred_element_type=jnp.float32,
            )
            out_ref[:, inner * 128:(inner + 1) * 128] = filtered / fold_ref[...]


def moveout_stack(rows, matrices, taps, fold_share, length):
    sources, capacity, width = rows.shape
    bins = fold_share.shape[0]
    classes, groups = matrices.shape[0], matrices.shape[1]
    per_step = 4
    steps = groups // per_step
    return pl.pallas_call(
        moveout_kernel,
        grid=(steps + 1,),
        in_specs=[
            pl.BlockSpec((sources, capacity, width), lambda g: (0, 0, 0)),
            pl.BlockSpec(
                (classes, per_step, 256, 128), lambda g: (0, jnp.minimum(g, steps - 1), 0, 0)
            ),
            pl.BlockSpec((per_step, 256, 128), lambda g: (jnp.maximum(g - 1, 0), 0, 0)),
            pl.BlockSpec((bins, 1), lambda g: (0, 0)),
        ],
        out_specs=pl.BlockSpec((bins, per_step * 128), lambda g: (0, jnp.maximum(g - 1, 0))),
        out_shape=jax.ShapeDtypeStruct((bins, length), jnp.float32),
        scratch_shapes=[
            pltpu.VMEM((classes * 2 * bins, width), jnp.bfloat16),
            pltpu.VMEM((bins, length + 256), jnp.float32),
        ],
    )(rows, matrices, taps, fold_share)


def filter_matrix(taps):
    taps_count, length = taps.shape
    groups = length // 128
    half = (taps_count - 1) // 2
    span = 384
    placed = taps.T.reshape(groups, 128, taps_count)
    lead = PAD - half
    placed = jnp.pad(placed, ((0, 0), (0, 0), (lead, span - taps_count - lead)))
    flat = placed.reshape(groups, 128 * span)[:, : 128 * (span - 1)]
    skewed = flat.reshape(groups, 128, span - 1)[:, :, :256]
    return jnp.transpose(skewed, (0, 2, 1))


def send_kernel(line_ref, bin_ref, offset_ref, traces_ref, out_ref, *, bins, tiles):
    dests, capacity, width = out_ref.shape
    trace_count, length = traces_ref.shape
    slots = dests * capacity
    block = trace_count // offset_ref.shape[0]
    line_id = line_ref[...].reshape(trace_count, 1)
    bin_id = bin_ref[...].reshape(trace_count, 1)
    trace_index = lax.broadcasted_iota(jnp.int32, (trace_count, 1), 0)
    class_id = jnp.zeros((trace_count, 1), jnp.int32)
    for block_index in range(offset_ref.shape[0]):
        class_id = jnp.where(trace_index // block == block_index, offset_ref[block_index], class_id)
    line_row = line_ref[...].reshape(1, trace_count)
    bin_row = bin_ref[...].reshape(1, trace_count)
    dest_row = line_row * tiles + bin_row // bins
    onehot = (lax.broadcasted_iota(jnp.int32, (dests, trace_count), 0) == dest_row).astype(
        jnp.bfloat16
    )
    row = lax.broadcasted_iota(jnp.int32, (trace_count, trace_count), 0)
    col = lax.broadcasted_iota(jnp.int32, (trace_count, trace_count), 1)
    upper = (row <= col).astype(jnp.bfloat16)
    running = jnp.dot(onehot, upper, preferred_element_type=jnp.float32)
    rank = jnp.sum(running * onehot.astype(jnp.float32), axis=0, keepdims=True) - 1.0
    slot = dest_row.astype(jnp.float32) * capacity + rank
    wanted = lax.broadcasted_iota(jnp.int32, (slots, trace_count), 0).astype(jnp.float32)
    select = (wanted == slot).astype(jnp.bfloat16)
    lane = lax.broadcasted_iota(jnp.int32, (trace_count, width - length), 1)
    meta = jnp.where(
        lane == 0, bin_id % bins, jnp.where(lane == 1, class_id, jnp.where(lane == 2, 1, 0))
    ).astype(jnp.bfloat16)
    rows = jnp.dot(select, traces_ref[...], preferred_element_type=jnp.float32)
    meta_rows = jnp.dot(select, meta, preferred_element_type=jnp.float32)
    out_ref[:, :, :length] = rows.astype(jnp.bfloat16).reshape(dests, capacity, length)
    out_ref[:, :, length:] = meta_rows.astype(jnp.bfloat16).reshape(dests, capacity, width - length)


def build_send(trace_line, trace_bin, block_offset, traces, dests, capacity, bins, tiles):
    trace_count, length = traces.shape
    width = length + META
    in_vmem = pl.BlockSpec(memory_space=pltpu.VMEM)
    return pl.pallas_call(
        functools.partial(send_kernel, bins=bins, tiles=tiles),
        in_specs=[in_vmem, in_vmem, pl.BlockSpec(memory_space=pltpu.SMEM), in_vmem],
        out_shape=jax.ShapeDtypeStruct((dests, capacity, width), jnp.bfloat16),
    )(trace_line, trace_bin, block_offset, traces)


def body(traces, trace_line, trace_bin, block_offset, nmo_coef, band_shift, bandpass, fold):
    line_count = lax.axis_size("line")
    tile_count = lax.axis_size("tile")
    trace_count, length = traces.shape
    block_rows = trace_count // block_offset.shape[0]
    bin_share = fold.shape[1]
    dest_count = line_count * tile_count
    capacity = 4
    slots = dest_count * capacity
    send = build_send(
        trace_line, trace_bin, block_offset, traces, dest_count, capacity, bin_share, tile_count
    )
    received = lax.all_to_all(
        send,
        ("line", "tile"),
        split_axis=0,
        concat_axis=0,
        tiled=True,
    )
    matrices = jnp.stack(
        [
            moveout_matrix(nmo_coef[0, offset_index], band_shift[0, offset_index])
            for offset_index in range(nmo_coef.shape[1])
        ]
    )
    fold_share = fold[0].astype(jnp.float32)[:, None]
    filtered = moveout_stack(received, matrices, filter_matrix(bandpass), fold_share, length)
    return filtered[None]


def solution(mesh):
    placed = (
        P(("line", "tile"), None),
        P(("line", "tile")),
        P(("line", "tile")),
        P(("line", "tile")),
        P("line", None, None, None),
        P("line", None, None),
        P(),
        P("line", "tile"),
    )
    return jax.shard_map(
        body, mesh=mesh, in_specs=placed, out_specs=P("line", "tile", None), check_vma=False
    )
```

```python
import functools

import jax
import jax.numpy as jnp
from jax import lax
from jax.sharding import PartitionSpec as P
from jax.experimental import pallas as pl
from jax.experimental.pallas import tpu as pltpu

META = 128
PAD = 16


def moveout_matrix(coef_rows, shift_rows):
    taps_count = coef_rows.shape[0]
    groups = coef_rows.shape[1] // 128
    column = jnp.arange(128, dtype=jnp.int32).reshape(1, 1, 128)
    position = jnp.arange(256, dtype=jnp.int32).reshape(1, 256, 1)
    shifts = shift_rows.reshape(groups, 1, 128)
    weights = coef_rows.astype(jnp.float32).reshape(taps_count, groups, 1, 128)
    matrix = jnp.zeros((groups, 256, 128), jnp.float32)
    for tap_index in range(taps_count):
        matrix = matrix + jnp.where(
            position == column + shifts + tap_index, weights[tap_index], 0.0
        )
    return matrix.astype(jnp.bfloat16)


def moveout_kernel(rows_ref, matrix_ref, taps_ref, fold_ref, out_ref, part_ref, stack_ref):
    step = pl.program_id(0)
    last = pl.num_programs(0) - 1
    classes, per_step = matrix_ref.shape[0], matrix_ref.shape[1]
    bins, length = stack_ref.shape[0], stack_ref.shape[1] - 256
    sources, capacity, width = rows_ref.shape
    slot_count = sources * capacity

    @pl.when(step == 0)
    def _():
        stack_ref[:, :128] = jnp.zeros((bins, 128), jnp.float32)
        stack_ref[:, length + 128:] = jnp.zeros((bins, 128), jnp.float32)
        rows_all = rows_ref[...].reshape(slot_count, width)
        meta = rows_all[:, length:].astype(jnp.float32).T
        key = jnp.where(meta[2:3, :] == 1.0, meta[1:2, :] * bins + meta[0:1, :], -1.0)
        keys = lax.broadcasted_iota(jnp.int32, (classes * bins, slot_count), 0).astype(jnp.float32)
        select = (keys == key).astype(jnp.bfloat16)
        summed = jnp.dot(select, rows_all[:, :length], preferred_element_type=jnp.float32)
        high = summed.astype(jnp.bfloat16)
        middle = (summed - high.astype(jnp.float32)).astype(jnp.bfloat16)
        for offset_index in range(classes):
            base = offset_index * 2 * bins
            part_ref[base:base + bins, :length] = high[offset_index * bins:(offset_index + 1) * bins]
            part_ref[base + bins:base + 2 * bins, :length] = middle[
                offset_index * bins:(offset_index + 1) * bins
            ]
        part_ref[:, length:] = jnp.zeros((classes * 2 * bins, width - length), jnp.bfloat16)

    @pl.when(step < last)
    def _():
        for inner in range(per_step):
            start = pl.multiple_of((step * per_step + inner) * 128, 128)
            total = jnp.zeros((bins, 128), jnp.float32)
            for offset_index in range(classes):
                base = offset_index * 2 * bins
                window = part_ref[base:base + 2 * bins, pl.ds(start, 256)]
                product = jnp.dot(
                    window, matrix_ref[offset_index, inner], preferred_element_type=jnp.float32
                )
                total = total + product[:bins] + product[bins:]
            stack_ref[:, pl.ds(start + 128, 128)] = total

    @pl.when(step > 0)
    def _():
        for inner in range(per_step):
            start = pl.multiple_of(((step - 1) * per_step + inner) * 128, 128)
            window = stack_ref[:, pl.ds(start, 384)][:, 128 - PAD:384 - PAD]
            filtered = jnp.dot(
                window,
                taps_ref[inner],
                precision=lax.Precision.HIGHEST,
                preferred_element_type=jnp.float32,
            )
            out_ref[:, inner * 128:(inner + 1) * 128] = filtered / fold_ref[...]


def moveout_stack(rows, matrices, taps, fold_share, length):
    sources, capacity, width = rows.shape
    bins = fold_share.shape[0]
    classes, groups = matrices.shape[0], matrices.shape[1]
    per_step = 4
    steps = groups // per_step
    return pl.pallas_call(
        moveout_kernel,
        grid=(steps + 1,),
        in_specs=[
            pl.BlockSpec((sources, capacity, width), lambda g: (0, 0, 0)),
            pl.BlockSpec(
                (classes, per_step, 256, 128), lambda g: (0, jnp.minimum(g, steps - 1), 0, 0)
            ),
            pl.BlockSpec((per_step, 256, 128), lambda g: (jnp.maximum(g - 1, 0), 0, 0)),
            pl.BlockSpec((bins, 1), lambda g: (0, 0)),
        ],
        out_specs=pl.BlockSpec((bins, per_step * 128), lambda g: (0, jnp.maximum(g - 1, 0))),
        out_shape=jax.ShapeDtypeStruct((bins, length), jnp.float32),
        scratch_shapes=[
            pltpu.VMEM((classes * 2 * bins, width), jnp.bfloat16),
            pltpu.VMEM((bins, length + 256), jnp.float32),
        ],
    )(rows, matrices, taps, fold_share)


def filter_matrix(taps):
    taps_count, length = taps.shape
    groups = length // 128
    half = (taps_count - 1) // 2
    span = 384
    placed = taps.T.reshape(groups, 128, taps_count)
    lead = PAD - half
    placed = jnp.pad(placed, ((0, 0), (0, 0), (lead, span - taps_count - lead)))
    flat = placed.reshape(groups, 128 * span)[:, : 128 * (span - 1)]
    skewed = flat.reshape(groups, 128, span - 1)[:, :, :256]
    return jnp.transpose(skewed, (0, 2, 1))


def send_kernel(line_ref, bin_ref, offset_ref, traces_ref, out_ref, *, bins, tiles):
    dests, capacity, width = out_ref.shape
    trace_count, length = traces_ref.shape
    slots = dests * capacity
    block = trace_count // offset_ref.shape[0]
    line_id = line_ref[...].reshape(trace_count, 1)
    bin_id = bin_ref[...].reshape(trace_count, 1)
    trace_index = lax.broadcasted_iota(jnp.int32, (trace_count, 1), 0)
    class_id = jnp.zeros((trace_count, 1), jnp.int32)
    for block_index in range(offset_ref.shape[0]):
        class_id = jnp.where(trace_index // block == block_index, offset_ref[block_index], class_id)
    line_row = line_ref[...].reshape(1, trace_count)
    bin_row = bin_ref[...].reshape(1, trace_count)
    dest_row = (bin_row // bins) * (dests // tiles) + line_row
    onehot = (lax.broadcasted_iota(jnp.int32, (dests, trace_count), 0) == dest_row).astype(
        jnp.bfloat16
    )
    row = lax.broadcasted_iota(jnp.int32, (trace_count, trace_count), 0)
    col = lax.broadcasted_iota(jnp.int32, (trace_count, trace_count), 1)
    upper = (row <= col).astype(jnp.bfloat16)
    running = jnp.dot(onehot, upper, preferred_element_type=jnp.float32)
    rank = jnp.sum(running * onehot.astype(jnp.float32), axis=0, keepdims=True) - 1.0
    slot = dest_row.astype(jnp.float32) * capacity + rank
    wanted = lax.broadcasted_iota(jnp.int32, (slots, trace_count), 0).astype(jnp.float32)
    select = (wanted == slot).astype(jnp.bfloat16)
    lane = lax.broadcasted_iota(jnp.int32, (trace_count, width - length), 1)
    meta = jnp.where(
        lane == 0, bin_id % bins, jnp.where(lane == 1, class_id, jnp.where(lane == 2, 1, 0))
    ).astype(jnp.bfloat16)
    rows = jnp.dot(select, traces_ref[...], preferred_element_type=jnp.float32)
    meta_rows = jnp.dot(select, meta, preferred_element_type=jnp.float32)
    out_ref[:, :, :length] = rows.astype(jnp.bfloat16).reshape(dests, capacity, length)
    out_ref[:, :, length:] = meta_rows.astype(jnp.bfloat16).reshape(dests, capacity, width - length)


def build_send(trace_line, trace_bin, block_offset, traces, dests, capacity, bins, tiles):
    trace_count, length = traces.shape
    width = length + META
    in_vmem = pl.BlockSpec(memory_space=pltpu.VMEM)
    return pl.pallas_call(
        functools.partial(send_kernel, bins=bins, tiles=tiles),
        in_specs=[in_vmem, in_vmem, pl.BlockSpec(memory_space=pltpu.SMEM), in_vmem],
        out_shape=jax.ShapeDtypeStruct((dests, capacity, width), jnp.bfloat16),
    )(trace_line, trace_bin, block_offset, traces)


def body(traces, trace_line, trace_bin, block_offset, nmo_coef, band_shift, bandpass, fold):
    line_count = lax.axis_size("line")
    tile_count = lax.axis_size("tile")
    trace_count, length = traces.shape
    block_rows = trace_count // block_offset.shape[0]
    bin_share = fold.shape[1]
    dest_count = line_count * tile_count
    capacity = 4
    slots = dest_count * capacity
    send = build_send(
        trace_line, trace_bin, block_offset, traces, dest_count, capacity, bin_share, tile_count
    )
    received = lax.all_to_all(
        send,
        ("tile", "line"),
        split_axis=0,
        concat_axis=0,
        tiled=True,
    )
    matrices = jnp.stack(
        [
            moveout_matrix(nmo_coef[0, offset_index], band_shift[0, offset_index])
            for offset_index in range(nmo_coef.shape[1])
        ]
    )
    fold_share = fold[0].astype(jnp.float32)[:, None]
    filtered = moveout_stack(received, matrices, filter_matrix(bandpass), fold_share, length)
    return filtered[None]


def solution(mesh):
    placed = (
        P(("line", "tile"), None),
        P(("line", "tile")),
        P(("line", "tile")),
        P(("line", "tile")),
        P("line", None, None, None),
        P("line", None, None),
        P(),
        P("line", "tile"),
    )
    return jax.shard_map(
        body, mesh=mesh, in_specs=placed, out_specs=P("line", "tile", None), check_vma=False
    )
```

```python
import functools

import jax
import jax.numpy as jnp
from jax import lax
from jax.sharding import PartitionSpec as P
from jax.experimental import pallas as pl
from jax.experimental.pallas import tpu as pltpu

META = 128
PAD = 16
BAND = 160


def moveout_matrix(coef_rows, shift_rows):
    taps_count = coef_rows.shape[0]
    groups = coef_rows.shape[1] // 128
    column = jnp.arange(128, dtype=jnp.int32).reshape(1, 1, 128)
    position = jnp.arange(256, dtype=jnp.int32).reshape(1, 256, 1)
    shifts = shift_rows.reshape(groups, 1, 128)
    weights = coef_rows.astype(jnp.float32).reshape(taps_count, groups, 1, 128)
    matrix = jnp.zeros((groups, 256, 128), jnp.float32)
    for tap_index in range(taps_count):
        matrix = matrix + jnp.where(
            position == column + shifts + tap_index, weights[tap_index], 0.0
        )
    return matrix.astype(jnp.bfloat16)


def moveout_kernel(rows_ref, matrix_ref, taps_ref, fold_ref, out_ref, part_ref, stack_ref):
    step = pl.program_id(0)
    last = pl.num_programs(0) - 1
    classes, per_step = matrix_ref.shape[0], matrix_ref.shape[1]
    bins, length = stack_ref.shape[0], stack_ref.shape[1] - 256
    sources, capacity, width = rows_ref.shape
    slot_count = sources * capacity

    @pl.when(step == 0)
    def _():
        stack_ref[:, :128] = jnp.zeros((bins, 128), jnp.float32)
        stack_ref[:, length + 128:] = jnp.zeros((bins, 128), jnp.float32)
        rows_all = rows_ref[...].reshape(slot_count, width)
        meta = rows_all[:, length:].astype(jnp.float32).T
        key = jnp.where(meta[2:3, :] == 1.0, meta[1:2, :] * bins + meta[0:1, :], -1.0)
        keys = lax.broadcasted_iota(jnp.int32, (classes * bins, slot_count), 0).astype(jnp.float32)
        select = (keys == key).astype(jnp.bfloat16)
        summed = jnp.dot(select, rows_all[:, :length], preferred_element_type=jnp.float32)
        high = summed.astype(jnp.bfloat16)
        middle = (summed - high.astype(jnp.float32)).astype(jnp.bfloat16)
        for offset_index in range(classes):
            base = offset_index * 2 * bins
            part_ref[base:base + bins, :length] = high[offset_index * bins:(offset_index + 1) * bins]
            part_ref[base + bins:base + 2 * bins, :length] = middle[
                offset_index * bins:(offset_index + 1) * bins
            ]
        part_ref[:, length:] = jnp.zeros((classes * 2 * bins, width - length), jnp.bfloat16)

    @pl.when(step < last)
    def _():
        for inner in range(per_step):
            start = pl.multiple_of((step * per_step + inner) * 128, 128)
            total = jnp.zeros((bins, 128), jnp.float32)
            for offset_index in range(classes):
                base = offset_index * 2 * bins
                window = part_ref[base:base + 2 * bins, pl.ds(start, 256)]
                product = jnp.dot(
                    window, matrix_ref[offset_index, inner], preferred_element_type=jnp.float32
                )
                total = total + product[:bins] + product[bins:]
            stack_ref[:, pl.ds(start + 128, 128)] = total

    @pl.when(step > 0)
    def _():
        for inner in range(per_step):
            start = pl.multiple_of(((step - 1) * per_step + inner) * 128, 128)
            window = stack_ref[:, pl.ds(start, 384)][:, 128 - PAD:128 - PAD + BAND]
            filtered = jnp.dot(
                window,
                taps_ref[inner],
                precision=lax.Precision.HIGHEST,
                preferred_element_type=jnp.float32,
            )
            out_ref[:, inner * 128:(inner + 1) * 128] = filtered / fold_ref[...]


def moveout_stack(rows, matrices, taps, fold_share, length):
    sources, capacity, width = rows.shape
    bins = fold_share.shape[0]
    classes, groups = matrices.shape[0], matrices.shape[1]
    per_step = 8
    steps = groups // per_step
    return pl.pallas_call(
        moveout_kernel,
        grid=(steps + 1,),
        in_specs=[
            pl.BlockSpec((sources, capacity, width), lambda g: (0, 0, 0)),
            pl.BlockSpec(
                (classes, per_step, 256, 128), lambda g: (0, jnp.minimum(g, steps - 1), 0, 0)
            ),
            pl.BlockSpec((per_step, BAND, 128), lambda g: (jnp.maximum(g - 1, 0), 0, 0)),
            pl.BlockSpec((bins, 1), lambda g: (0, 0)),
        ],
        out_specs=pl.BlockSpec((bins, per_step * 128), lambda g: (0, jnp.maximum(g - 1, 0))),
        out_shape=jax.ShapeDtypeStruct((bins, length), jnp.float32),
        scratch_shapes=[
            pltpu.VMEM((classes * 2 * bins, width), jnp.bfloat16),
            pltpu.VMEM((bins, length + 256), jnp.float32),
        ],
    )(rows, matrices, taps, fold_share)


def filter_matrix(taps):
    taps_count, length = taps.shape
    groups = length // 128
    half = (taps_count - 1) // 2
    span = 384
    placed = taps.T.reshape(groups, 128, taps_count)
    lead = PAD - half
    placed = jnp.pad(placed, ((0, 0), (0, 0), (lead, span - taps_count - lead)))
    flat = placed.reshape(groups, 128 * span)[:, : 128 * (span - 1)]
    skewed = flat.reshape(groups, 128, span - 1)[:, :, :BAND]
    return jnp.transpose(skewed, (0, 2, 1))


def send_kernel(line_ref, bin_ref, offset_ref, traces_ref, out_ref, *, bins, tiles):
    dests, capacity, width = out_ref.shape
    trace_count, length = traces_ref.shape
    slots = dests * capacity
    block = trace_count // offset_ref.shape[0]
    line_id = line_ref[...].reshape(trace_count, 1)
    bin_id = bin_ref[...].reshape(trace_count, 1)
    trace_index = lax.broadcasted_iota(jnp.int32, (trace_count, 1), 0)
    class_id = jnp.zeros((trace_count, 1), jnp.int32)
    for block_index in range(offset_ref.shape[0]):
        class_id = jnp.where(trace_index // block == block_index, offset_ref[block_index], class_id)
    line_row = line_ref[...].reshape(1, trace_count)
    bin_row = bin_ref[...].reshape(1, trace_count)
    dest_row = (bin_row // bins) * (dests // tiles) + line_row
    onehot = (lax.broadcasted_iota(jnp.int32, (dests, trace_count), 0) == dest_row).astype(
        jnp.bfloat16
    )
    row = lax.broadcasted_iota(jnp.int32, (trace_count, trace_count), 0)
    col = lax.broadcasted_iota(jnp.int32, (trace_count, trace_count), 1)
    upper = (row <= col).astype(jnp.bfloat16)
    running = jnp.dot(onehot, upper, preferred_element_type=jnp.float32)
    rank = jnp.sum(running * onehot.astype(jnp.float32), axis=0, keepdims=True) - 1.0
    slot = dest_row.astype(jnp.float32) * capacity + rank
    wanted = lax.broadcasted_iota(jnp.int32, (slots, trace_count), 0).astype(jnp.float32)
    select = (wanted == slot).astype(jnp.bfloat16)
    lane = lax.broadcasted_iota(jnp.int32, (trace_count, width - length), 1)
    meta = jnp.where(
        lane == 0, bin_id % bins, jnp.where(lane == 1, class_id, jnp.where(lane == 2, 1, 0))
    ).astype(jnp.bfloat16)
    rows = jnp.dot(select, traces_ref[...], preferred_element_type=jnp.float32)
    meta_rows = jnp.dot(select, meta, preferred_element_type=jnp.float32)
    out_ref[:, :, :length] = rows.astype(jnp.bfloat16).reshape(dests, capacity, length)
    out_ref[:, :, length:] = meta_rows.astype(jnp.bfloat16).reshape(dests, capacity, width - length)


def build_send(trace_line, trace_bin, block_offset, traces, dests, capacity, bins, tiles):
    trace_count, length = traces.shape
    width = length + META
    in_vmem = pl.BlockSpec(memory_space=pltpu.VMEM)
    return pl.pallas_call(
        functools.partial(send_kernel, bins=bins, tiles=tiles),
        in_specs=[in_vmem, in_vmem, pl.BlockSpec(memory_space=pltpu.SMEM), in_vmem],
        out_shape=jax.ShapeDtypeStruct((dests, capacity, width), jnp.bfloat16),
    )(trace_line, trace_bin, block_offset, traces)


def body(traces, trace_line, trace_bin, block_offset, nmo_coef, band_shift, bandpass, fold):
    line_count = lax.axis_size("line")
    tile_count = lax.axis_size("tile")
    trace_count, length = traces.shape
    block_rows = trace_count // block_offset.shape[0]
    bin_share = fold.shape[1]
    dest_count = line_count * tile_count
    capacity = 4
    slots = dest_count * capacity
    send = build_send(
        trace_line, trace_bin, block_offset, traces, dest_count, capacity, bin_share, tile_count
    )
    received = lax.all_to_all(
        send,
        ("tile", "line"),
        split_axis=0,
        concat_axis=0,
        tiled=True,
    )
    matrices = jnp.stack(
        [
            moveout_matrix(nmo_coef[0, offset_index], band_shift[0, offset_index])
            for offset_index in range(nmo_coef.shape[1])
        ]
    )
    fold_share = fold[0].astype(jnp.float32)[:, None]
    filtered = moveout_stack(received, matrices, filter_matrix(bandpass), fold_share, length)
    return filtered[None]


def solution(mesh):
    placed = (
        P(("line", "tile"), None),
        P(("line", "tile")),
        P(("line", "tile")),
        P(("line", "tile")),
        P("line", None, None, None),
        P("line", None, None),
        P(),
        P("line", "tile"),
    )
    return jax.shard_map(
        body, mesh=mesh, in_specs=placed, out_specs=P("line", "tile", None), check_vma=False
    )
```

```python
import functools

import jax
import jax.numpy as jnp
from jax import lax
from jax.sharding import PartitionSpec as P
from jax.experimental import pallas as pl
from jax.experimental.pallas import tpu as pltpu

META = 128
PAD = 16
BAND = 160


def moveout_matrix(coef_rows, shift_rows):
    taps_count = coef_rows.shape[0]
    groups = coef_rows.shape[1] // 128
    column = jnp.arange(128, dtype=jnp.int32).reshape(1, 1, 128)
    position = jnp.arange(256, dtype=jnp.int32).reshape(1, 256, 1)
    shifts = shift_rows.reshape(groups, 1, 128)
    weights = coef_rows.astype(jnp.float32).reshape(taps_count, groups, 1, 128)
    matrix = jnp.zeros((groups, 256, 128), jnp.float32)
    for tap_index in range(taps_count):
        matrix = matrix + jnp.where(
            position == column + shifts + tap_index, weights[tap_index], 0.0
        )
    return matrix.astype(jnp.bfloat16)


def moveout_kernel(rows_ref, matrix_ref, taps_ref, fold_ref, out_ref, part_ref, stack_ref):
    step = pl.program_id(0)
    last = pl.num_programs(0) - 1
    classes, per_step = matrix_ref.shape[0], matrix_ref.shape[1]
    bins, length = stack_ref.shape[0], stack_ref.shape[1] - 256
    sources, capacity, width = rows_ref.shape
    slot_count = sources * capacity

    @pl.when(step == 0)
    def _():
        stack_ref[:, :128] = jnp.zeros((bins, 128), jnp.float32)
        stack_ref[:, length + 128:] = jnp.zeros((bins, 128), jnp.float32)
        rows_all = rows_ref[...].reshape(slot_count, width)
        meta = rows_all[:, length:].astype(jnp.float32).T
        key = jnp.where(meta[2:3, :] == 1.0, meta[1:2, :] * bins + meta[0:1, :], -1.0)
        keys = lax.broadcasted_iota(jnp.int32, (classes * bins, slot_count), 0).astype(jnp.float32)
        select = (keys == key).astype(jnp.bfloat16)
        summed = jnp.dot(select, rows_all[:, :length], preferred_element_type=jnp.float32)
        high = summed.astype(jnp.bfloat16)
        middle = (summed - high.astype(jnp.float32)).astype(jnp.bfloat16)
        for offset_index in range(classes):
            base = offset_index * 2 * bins
            part_ref[base:base + bins, :length] = high[offset_index * bins:(offset_index + 1) * bins]
            part_ref[base + bins:base + 2 * bins, :length] = middle[
                offset_index * bins:(offset_index + 1) * bins
            ]
        part_ref[:, length:] = jnp.zeros((classes * 2 * bins, width - length), jnp.bfloat16)

    @pl.when(step < last)
    def _():
        for inner in range(per_step):
            start = pl.multiple_of((step * per_step + inner) * 128, 128)
            total = jnp.zeros((bins, 128), jnp.float32)
            for offset_index in range(classes):
                base = offset_index * 2 * bins
                window = part_ref[base:base + 2 * bins, pl.ds(start, 256)]
                product = jnp.dot(
                    window, matrix_ref[offset_index, inner], preferred_element_type=jnp.float32
                )
                total = total + product[:bins] + product[bins:]
            stack_ref[:, pl.ds(start + 128, 128)] = total

    @pl.when(step > 0)
    def _():
        for inner in range(per_step):
            start = pl.multiple_of(((step - 1) * per_step + inner) * 128, 128)
            window = stack_ref[:, pl.ds(start, 384)][:, 128 - PAD:128 - PAD + BAND]
            filtered = jnp.dot(
                window,
                taps_ref[inner],
                precision=lax.Precision.HIGH,
                preferred_element_type=jnp.float32,
            )
            out_ref[:, inner * 128:(inner + 1) * 128] = filtered / fold_ref[...]


def moveout_stack(rows, matrices, taps, fold_share, length):
    sources, capacity, width = rows.shape
    bins = fold_share.shape[0]
    classes, groups = matrices.shape[0], matrices.shape[1]
    per_step = 8
    steps = groups // per_step
    return pl.pallas_call(
        moveout_kernel,
        grid=(steps + 1,),
        in_specs=[
            pl.BlockSpec((sources, capacity, width), lambda g: (0, 0, 0)),
            pl.BlockSpec(
                (classes, per_step, 256, 128), lambda g: (0, jnp.minimum(g, steps - 1), 0, 0)
            ),
            pl.BlockSpec((per_step, BAND, 128), lambda g: (jnp.maximum(g - 1, 0), 0, 0)),
            pl.BlockSpec((bins, 1), lambda g: (0, 0)),
        ],
        out_specs=pl.BlockSpec((bins, per_step * 128), lambda g: (0, jnp.maximum(g - 1, 0))),
        out_shape=jax.ShapeDtypeStruct((bins, length), jnp.float32),
        scratch_shapes=[
            pltpu.VMEM((classes * 2 * bins, width), jnp.bfloat16),
            pltpu.VMEM((bins, length + 256), jnp.float32),
        ],
    )(rows, matrices, taps, fold_share)


def filter_matrix(taps):
    taps_count, length = taps.shape
    groups = length // 128
    half = (taps_count - 1) // 2
    span = 384
    placed = taps.T.reshape(groups, 128, taps_count)
    lead = PAD - half
    placed = jnp.pad(placed, ((0, 0), (0, 0), (lead, span - taps_count - lead)))
    flat = placed.reshape(groups, 128 * span)[:, : 128 * (span - 1)]
    skewed = flat.reshape(groups, 128, span - 1)[:, :, :BAND]
    return jnp.transpose(skewed, (0, 2, 1))


def send_kernel(line_ref, bin_ref, offset_ref, traces_ref, out_ref, *, bins, tiles):
    dests, capacity, width = out_ref.shape
    trace_count, length = traces_ref.shape
    slots = dests * capacity
    block = trace_count // offset_ref.shape[0]
    line_id = line_ref[...].reshape(trace_count, 1)
    bin_id = bin_ref[...].reshape(trace_count, 1)
    trace_index = lax.broadcasted_iota(jnp.int32, (trace_count, 1), 0)
    class_id = jnp.zeros((trace_count, 1), jnp.int32)
    for block_index in range(offset_ref.shape[0]):
        class_id = jnp.where(trace_index // block == block_index, offset_ref[block_index], class_id)
    line_row = line_ref[...].reshape(1, trace_count)
    bin_row = bin_ref[...].reshape(1, trace_count)
    dest_row = (bin_row // bins) * (dests // tiles) + line_row
    onehot = (lax.broadcasted_iota(jnp.int32, (dests, trace_count), 0) == dest_row).astype(
        jnp.bfloat16
    )
    row = lax.broadcasted_iota(jnp.int32, (trace_count, trace_count), 0)
    col = lax.broadcasted_iota(jnp.int32, (trace_count, trace_count), 1)
    upper = (row <= col).astype(jnp.bfloat16)
    running = jnp.dot(onehot, upper, preferred_element_type=jnp.float32)
    rank = jnp.sum(running * onehot.astype(jnp.float32), axis=0, keepdims=True) - 1.0
    slot = dest_row.astype(jnp.float32) * capacity + rank
    wanted = lax.broadcasted_iota(jnp.int32, (slots, trace_count), 0).astype(jnp.float32)
    select = (wanted == slot).astype(jnp.bfloat16)
    lane = lax.broadcasted_iota(jnp.int32, (trace_count, width - length), 1)
    meta = jnp.where(
        lane == 0, bin_id % bins, jnp.where(lane == 1, class_id, jnp.where(lane == 2, 1, 0))
    ).astype(jnp.bfloat16)
    rows = jnp.dot(select, traces_ref[...], preferred_element_type=jnp.float32)
    meta_rows = jnp.dot(select, meta, preferred_element_type=jnp.float32)
    out_ref[:, :, :length] = rows.astype(jnp.bfloat16).reshape(dests, capacity, length)
    out_ref[:, :, length:] = meta_rows.astype(jnp.bfloat16).reshape(dests, capacity, width - length)


def build_send(trace_line, trace_bin, block_offset, traces, dests, capacity, bins, tiles):
    trace_count, length = traces.shape
    width = length + META
    in_vmem = pl.BlockSpec(memory_space=pltpu.VMEM)
    return pl.pallas_call(
        functools.partial(send_kernel, bins=bins, tiles=tiles),
        in_specs=[in_vmem, in_vmem, pl.BlockSpec(memory_space=pltpu.SMEM), in_vmem],
        out_shape=jax.ShapeDtypeStruct((dests, capacity, width), jnp.bfloat16),
    )(trace_line, trace_bin, block_offset, traces)


def body(traces, trace_line, trace_bin, block_offset, nmo_coef, band_shift, bandpass, fold):
    line_count = lax.axis_size("line")
    tile_count = lax.axis_size("tile")
    trace_count, length = traces.shape
    block_rows = trace_count // block_offset.shape[0]
    bin_share = fold.shape[1]
    dest_count = line_count * tile_count
    capacity = 4
    slots = dest_count * capacity
    send = build_send(
        trace_line, trace_bin, block_offset, traces, dest_count, capacity, bin_share, tile_count
    )
    received = lax.all_to_all(
        send,
        ("tile", "line"),
        split_axis=0,
        concat_axis=0,
        tiled=True,
    )
    matrices = jnp.stack(
        [
            moveout_matrix(nmo_coef[0, offset_index], band_shift[0, offset_index])
            for offset_index in range(nmo_coef.shape[1])
        ]
    )
    fold_share = fold[0].astype(jnp.float32)[:, None]
    filtered = moveout_stack(received, matrices, filter_matrix(bandpass), fold_share, length)
    return filtered[None]


def solution(mesh):
    placed = (
        P(("line", "tile"), None),
        P(("line", "tile")),
        P(("line", "tile")),
        P(("line", "tile")),
        P("line", None, None, None),
        P("line", None, None),
        P(),
        P("line", "tile"),
    )
    return jax.shard_map(
        body, mesh=mesh, in_specs=placed, out_specs=P("line", "tile", None), check_vma=False
    )
```
